32 devices in a mesh: sea: 8 (over z, y), tm: 4 (over x, core).
Axes of the slice: x: 2, y: 2, z: 4, core: 2. Of those that a mesh axis runs over, the one named last changes fastest.
Arguments:
- motion: bfloat16 [4096, 64, 256], P('sea', 'tm'), may hold values from -6 to 6
- kappa: float32 [4096], P('sea'), may hold values from 0.2 to 5
- react: float32 [4096], P('sea'), may hold values from 0.02 to 0.5
- green: bfloat16 [64, 2, 512, 4096], P('tm', None, None, 'sea'), may hold values from -0.09375 to 0.09375
Outputs:
- prior_part: bfloat16 [4096, 64, 256], P('sea', 'tm')
- sensor_data: float32 [512, 64, 2, 256], P('sea', 'tm')
The draws below stay inside these ranges and needn't reach their ends.
All inputs are finite; a program needn't handle non-finite values.
Results may differ from the reference program's by a relative error of at most 0.01295.
Values may be sent and summed in bfloat16 or wider, within the bound.
No kernel may reach another device: no remote copies, remote signals or barrier semaphores. Data moves between devices by JAX's collectives and lax.ppermute only.
A program may use at most 192 MiB of HBM per device.

```python
import math
import jax
import jax.numpy as jnp
from jax import lax

P_DEV = 512
COLS = 256
TIMES = 64
SENSORS = 512
SWEEPS = 6
POINTS = 4096
N_SEA = 8


def spiked(values, rng, source, target, blocks, factor):
    def block_of(dim):
        return (jnp.arange(values.shape[dim]) // (values.shape[dim] // blocks)).reshape((-1,) + (1,) * (values.ndim - 1 - dim))

    first = jax.random.permutation(rng, blocks)[block_of(target)]
    other_side = (block_of(target) + blocks // 2) % blocks
    return jnp.where((block_of(source) == first) | (block_of(source) == other_side), factor * values, values)


def steps_of(own_key, shape, cuts, low, high):
    factor_of = 1.0
    for axis_at, shards_of in cuts:
        heights = jax.random.uniform(jax.random.fold_in(jax.random.fold_in(own_key, 6), axis_at), (shards_of,), jnp.float32, low / len(cuts), high / len(cuts))
        factor_of = factor_of * jnp.repeat(jnp.exp(heights), shape[axis_at] // shards_of).reshape((-1,) + (1,) * (len(shape) - 1 - axis_at))
    return factor_of


def centred(stream_key, dims, scale, most, pieces=(), kind=jnp.bfloat16):
    gain = steps_of(stream_key, dims, pieces, -0.22, 0.18) if pieces else 1.0
    entries = jax.random.normal(stream_key, dims, jnp.float32) * scale * gain
    return jnp.minimum(jnp.maximum(entries, -most), most).astype(kind)


def gaussian_with(own_key, extent, width, reach, cuts, heavy, kind=jnp.bfloat16):
    result = width * jax.random.normal(own_key, extent, jnp.float32)
    if cuts:
        result = result * steps_of(own_key, extent, cuts, -0.22, 0.18)
    return jnp.clip(spiked(result, jax.random.fold_in(own_key, 3), *heavy), -reach, reach).astype(kind)


def setup_inputs(seed: int = 0) -> dict:
    splits = jax.random.split(jax.random.key(seed), 5)
    motion = centred(splits[0], (POINTS, TIMES, COLS), 1.0, 6.0, ((0, 8), (1, 4)))
    kappa = jnp.clip(jnp.exp(math.log(5.0) - 3.218876 * jax.random.uniform(splits[1], (POINTS,), jnp.float32) ** steps_of(splits[1], (POINTS,), ((0, 8),), -0.2, 0.2)), 0.2, 5.0)
    react = jnp.clip(jnp.exp(math.log(0.5) - 3.218876 * jax.random.uniform(splits[2], (POINTS,), jnp.float32) ** steps_of(splits[2], (POINTS,), ((0, 8),), -0.2, 0.2)), 0.02, 0.5)
    green = gaussian_with(splits[3], (TIMES, 2, SENSORS, POINTS), (2 * P_DEV * N_SEA) ** -0.5, 0.09375, ((0, 4), (3, 8)), (3, 2, 8, 2.0))
    return dict(motion=motion, kappa=kappa, react=react, green=green)


def omega_table():
    return [1.0 / (1.05 + 0.95 * math.cos((2 * k + 1) * math.pi / (2 * SWEEPS))) for k in range(SWEEPS)]

def reference(motion, kappa, react, green):
    zero_one = jnp.zeros((1,), jnp.float32)
    left_k = jnp.concatenate([zero_one, kappa[:-1]])
    right_k = jnp.concatenate([kappa[:-1], zero_one])
    diag = left_k + right_k + react
    weights = omega_table()

    def smooth(slab):
        state = jnp.zeros_like(slab)
        for k in range(SWEEPS):
            padded = jnp.pad(state, ((1, 1), (0, 0)))
            applied = diag[:, None] * state - left_k[:, None] * padded[:-2] - right_k[:, None] * padded[2:]
            state = state + weights[k] * (slab - applied) / diag[:, None]
        return state
    fields = lax.map(smooth, jnp.moveaxis(motion.astype(jnp.float32), 1, 0))
    prior_part = jnp.moveaxis(fields, 0, 1).astype(jnp.bfloat16)
    scale = 1.0 / math.sqrt(TIMES)

    def group_step(total, group):
        start = (group * P_DEV).astype(jnp.int32)
        block = lax.dynamic_slice_in_dim(prior_part, start, P_DEV, 0).astype(jnp.float32)
        spec = jnp.fft.fft(block, axis=1) * scale
        parts = jnp.stack([jnp.real(spec), jnp.imag(spec)])
        parts = jnp.transpose(parts, (2, 0, 1, 3)).astype(jnp.bfloat16)
        block_green = lax.dynamic_slice_in_dim(green, start, P_DEV, 3).astype(jnp.float32)
        prods = jnp.einsum('fksp,fjpc->sfkjc', block_green, parts.astype(jnp.float32))
        real_part = prods[:, :, 0, 0] - prods[:, :, 1, 1]
        imag_part = prods[:, :, 0, 1] + prods[:, :, 1, 0]
        partial_value = jnp.stack([real_part, imag_part], axis=2).astype(jnp.bfloat16)
        partial_value = lax.optimization_barrier(partial_value)
        return (total + partial_value.astype(jnp.float32), None)
    start_total = jnp.zeros((SENSORS, TIMES, 2, COLS), jnp.float32)
    sensor_data, unused = lax.scan(group_step, start_total, jnp.arange(N_SEA, dtype=jnp.int32))
    return (prior_part, sensor_data)
```

```python
import math

import jax
import jax.numpy as jnp
from jax import lax
from jax.sharding import PartitionSpec as P

SWEEPS = 6
CHUNKS = 2


def from_left(block, axis):
    count = lax.axis_size(axis)
    return lax.ppermute(block, axis, [(i, i + 1) for i in range(count - 1)])


def from_right(block, axis):
    count = lax.axis_size(axis)
    return lax.ppermute(block, axis, [(i + 1, i) for i in range(count - 1)])


def omega_table(count):
    return [
        1.0 / (1.05 + 0.95 * math.cos((2 * k + 1) * math.pi / (2 * count))) for k in range(count)
    ]


def extended_coefficients(kappa, react, halo):
    points = kappa.shape[0]
    groups = lax.axis_size("sea")
    total_points = points * groups
    where_sea = lax.axis_index("sea")
    kappa_ext = jnp.concatenate(
        [from_left(kappa[points - halo - 1 :], "sea"), kappa, from_right(kappa[:halo], "sea")]
    )
    react_ext = jnp.concatenate(
        [from_left(react[points - halo :], "sea"), react, from_right(react[:halo], "sea")]
    )
    index = where_sea * points - halo + jnp.arange(points + 2 * halo, dtype=jnp.int32)
    valid = (index >= 0) & (index < total_points)
    left_k = jnp.where(valid & (index >= 1), kappa_ext[:-1], 0.0)
    right_k = jnp.where(valid & (index < total_points - 1), kappa_ext[1:], 0.0)
    react_v = jnp.where(valid, react_ext, 1.0)
    diag = left_k + right_k + react_v
    return left_k[:, None, None], right_k[:, None, None], diag[:, None, None]


def smooth(source, left_k, right_k, diag, halo):
    weights = omega_table(SWEEPS)
    state = weights[0] * source / diag
    for k in range(1, SWEEPS):
        padded = jnp.pad(state, ((1, 1), (0, 0), (0, 0)))
        applied = diag * state - left_k * padded[:-2] - right_k * padded[2:]
        state = state + weights[k] * (source - applied) / diag
    return state[halo : state.shape[0] - halo]


def dft_tables(steps_all):
    freq_ids = jnp.arange(steps_all, dtype=jnp.int32)
    phase_ids = freq_ids[:, None] * freq_ids[None, :] % steps_all
    angles = phase_ids.astype(jnp.float32) * (2.0 * math.pi / steps_all)
    scale = 1.0 / math.sqrt(steps_all)
    table = jnp.stack([jnp.cos(angles) * scale, -jnp.sin(angles) * scale], axis=1)
    table_high = lax.optimization_barrier(table.astype(jnp.bfloat16))
    table_low = (table - table_high.astype(jnp.float32)).astype(jnp.bfloat16)
    return table_high, table_low


def forward_chunk(prior_part, green, table_high, table_low):
    piece = lax.all_to_all(prior_part, "tm", split_axis=0, concat_axis=1, tiled=True)
    spectrum = jnp.einsum("fkt,ptc->fkpc", table_high, piece, preferred_element_type=jnp.float32)
    spectrum = spectrum + jnp.einsum(
        "fkt,ptc->fkpc", table_low, piece, preferred_element_type=jnp.float32
    )
    spectrum = spectrum.astype(jnp.bfloat16)
    spectra = lax.all_to_all(spectrum, "tm", split_axis=0, concat_axis=2, tiled=True)
    real_s = spectra[:, 0]
    imag_s = spectra[:, 1]
    mixed = jnp.stack(
        [jnp.stack([real_s, imag_s], axis=2), jnp.stack([-imag_s, real_s], axis=2)], axis=1
    )
    partial = jnp.einsum("fksp,fkprc->sfrc", green, mixed, preferred_element_type=jnp.float32)
    return lax.psum_scatter(
        partial.astype(jnp.bfloat16), "sea", scatter_dimension=0, tiled=True
    ).astype(jnp.float32)


def on_device(motion, kappa, react, green):
    halo = SWEEPS - 1
    cols = motion.shape[2]
    width = cols // CHUNKS
    left_k, right_k, diag = extended_coefficients(kappa, react, halo)
    motion_ext = jnp.concatenate(
        [from_left(motion[motion.shape[0] - halo :], "sea"), motion, from_right(motion[:halo], "sea")]
    )
    table_high, table_low = dft_tables(motion.shape[1] * lax.axis_size("tm"))
    priors = []
    sensors = []
    for c in range(CHUNKS):
        source = motion_ext[:, :, c * width : (c + 1) * width].astype(jnp.float32)
        prior_part = smooth(source, left_k, right_k, diag, halo).astype(jnp.bfloat16)
        priors.append(prior_part)
        sensors.append(forward_chunk(prior_part, green, table_high, table_low))
    return (jnp.concatenate(priors, axis=2), jnp.concatenate(sensors, axis=3))


def solution(mesh):
    in_specs = (P("sea", "tm", None), P("sea"), P("sea"), P("tm", None, None, "sea"))
    out_specs = (P("sea", "tm", None), P("sea", "tm", None, None))
    return jax.shard_map(
        on_device, mesh=mesh, in_specs=in_specs, out_specs=out_specs, check_vma=False
    )
```

```python
import math

import jax
import jax.numpy as jnp
from jax import lax
from jax.sharding import PartitionSpec as P

SWEEPS = 6
CHUNKS = 2


def from_left(block, axis):
    count = lax.axis_size(axis)
    return lax.ppermute(block, axis, [(i, i + 1) for i in range(count - 1)])


def from_right(block, axis):
    count = lax.axis_size(axis)
    return lax.ppermute(block, axis, [(i + 1, i) for i in range(count - 1)])


def omega_table(count):
    return [
        1.0 / (1.05 + 0.95 * math.cos((2 * k + 1) * math.pi / (2 * count))) for k in range(count)
    ]


def exchange_halo(motion, kappa, react, halo):
    points = motion.shape[0]
    shape = (halo,) + motion.shape[1:]
    size = math.prod(shape)
    tail = jnp.concatenate(
        [motion[points - halo :].astype(jnp.float32).reshape(-1), kappa[points - halo - 1 :], react[points - halo :]]
    )
    head = jnp.concatenate(
        [motion[:halo].astype(jnp.float32).reshape(-1), kappa[:halo], react[:halo]]
    )
    before = from_left(tail, "sea")
    after = from_right(head, "sea")
    motion_ext = jnp.concatenate(
        [before[:size].reshape(shape), motion.astype(jnp.float32), after[:size].reshape(shape)]
    )
    kappa_ext = jnp.concatenate([before[size : size + halo + 1], kappa, after[size : size + halo]])
    react_ext = jnp.concatenate([before[size + halo + 1 :], react, after[size + halo :]])
    return motion_ext, kappa_ext, react_ext


def extended_coefficients(kappa_ext, react_ext, points, halo):
    groups = lax.axis_size("sea")
    total_points = points * groups
    where_sea = lax.axis_index("sea")
    index = where_sea * points - halo + jnp.arange(points + 2 * halo, dtype=jnp.int32)
    valid = (index >= 0) & (index < total_points)
    left_k = jnp.where(valid & (index >= 1), kappa_ext[:-1], 0.0)
    right_k = jnp.where(valid & (index < total_points - 1), kappa_ext[1:], 0.0)
    react_v = jnp.where(valid, react_ext, 1.0)
    diag = left_k + right_k + react_v
    return left_k[:, None, None], right_k[:, None, None], diag[:, None, None]


def smooth(source, left_k, right_k, diag, halo):
    weights = omega_table(SWEEPS)
    state = weights[0] * source / diag
    for k in range(1, SWEEPS):
        padded = jnp.pad(state, ((1, 1), (0, 0), (0, 0)))
        applied = diag * state - left_k * padded[:-2] - right_k * padded[2:]
        state = state + weights[k] * (source - applied) / diag
    return state[halo : state.shape[0] - halo]


def dft_tables(steps_all):
    freq_ids = jnp.arange(steps_all, dtype=jnp.int32)
    phase_ids = freq_ids[:, None] * freq_ids[None, :] % steps_all
    angles = phase_ids.astype(jnp.float32) * (2.0 * math.pi / steps_all)
    scale = 1.0 / math.sqrt(steps_all)
    table = jnp.stack([jnp.cos(angles) * scale, -jnp.sin(angles) * scale], axis=1)
    table_high = lax.optimization_barrier(table.astype(jnp.bfloat16))
    table_low = (table - table_high.astype(jnp.float32)).astype(jnp.bfloat16)
    return table_high, table_low


def forward_chunk(prior_part, green, table_high, table_low):
    piece = lax.all_to_all(prior_part, "tm", split_axis=0, concat_axis=1, tiled=True)
    spectrum = jnp.einsum("fkt,ptc->fkpc", table_high, piece, preferred_element_type=jnp.float32)
    spectrum = spectrum + jnp.einsum(
        "fkt,ptc->fkpc", table_low, piece, preferred_element_type=jnp.float32
    )
    spectrum = spectrum.astype(jnp.bfloat16)
    spectra = lax.all_to_all(spectrum, "tm", split_axis=0, concat_axis=2, tiled=True)
    real_s = spectra[:, 0]
    imag_s = spectra[:, 1]
    mixed = jnp.stack(
        [jnp.stack([real_s, imag_s], axis=2), jnp.stack([-imag_s, real_s], axis=2)], axis=1
    )
    partial = jnp.einsum("fksp,fkprc->sfrc", green, mixed, preferred_element_type=jnp.float32)
    return lax.psum_scatter(
        partial.astype(jnp.bfloat16), "sea", scatter_dimension=0, tiled=True
    ).astype(jnp.float32)


def on_device(motion, kappa, react, green):
    halo = SWEEPS - 1
    cols = motion.shape[2]
    width = cols // CHUNKS
    motion_ext, kappa_ext, react_ext = exchange_halo(motion, kappa, react, halo)
    left_k, right_k, diag = extended_coefficients(kappa_ext, react_ext, motion.shape[0], halo)
    table_high, table_low = dft_tables(motion.shape[1] * lax.axis_size("tm"))
    priors = []
    sensors = []
    for c in range(CHUNKS):
        source = motion_ext[:, :, c * width : (c + 1) * width]
        if priors:
            source, _ = lax.optimization_barrier((source, priors[-1]))
        prior_part = smooth(source, left_k, right_k, diag, halo).astype(jnp.bfloat16)
        priors.append(prior_part)
        sensors.append(forward_chunk(prior_part, green, table_high, table_low))
    return (jnp.concatenate(priors, axis=2), jnp.concatenate(sensors, axis=3))


def solution(mesh):
    in_specs = (P("sea", "tm", None), P("sea"), P("sea"), P("tm", None, None, "sea"))
    out_specs = (P("sea", "tm", None), P("sea", "tm", None, None))
    return jax.shard_map(
        on_device, mesh=mesh, in_specs=in_specs, out_specs=out_specs, check_vma=False
    )
```

```python
import math

import jax
import jax.numpy as jnp
from jax import lax
from jax.sharding import PartitionSpec as P

SWEEPS = 6
CHUNKS = 2


def from_left(block, axis):
    count = lax.axis_size(axis)
    return lax.ppermute(block, axis, [(i, i + 1) for i in range(count - 1)])


def from_right(block, axis):
    count = lax.axis_size(axis)
    return lax.ppermute(block, axis, [(i + 1, i) for i in range(count - 1)])


def omega_table(count):
    return [
        1.0 / (1.05 + 0.95 * math.cos((2 * k + 1) * math.pi / (2 * count))) for k in range(count)
    ]


def exchange_halo(motion, kappa, react, halo):
    points = motion.shape[0]
    shape = (halo,) + motion.shape[1:]
    size = math.prod(shape)
    tail = jnp.concatenate(
        [motion[points - halo :].astype(jnp.float32).reshape(-1), kappa[points - halo - 1 :], react[points - halo :]]
    )
    head = jnp.concatenate(
        [motion[:halo].astype(jnp.float32).reshape(-1), kappa[:halo], react[:halo]]
    )
    before = from_left(tail, "sea")
    after = from_right(head, "sea")
    motion_ext = jnp.concatenate(
        [
            before[:size].reshape(shape).astype(motion.dtype),
            motion,
            after[:size].reshape(shape).astype(motion.dtype),
        ]
    )
    kappa_ext = jnp.concatenate([before[size : size + halo + 1], kappa, after[size : size + halo]])
    react_ext = jnp.concatenate([before[size + halo + 1 :], react, after[size + halo :]])
    return motion_ext, kappa_ext, react_ext


def extended_coefficients(kappa_ext, react_ext, points, halo):
    groups = lax.axis_size("sea")
    total_points = points * groups
    where_sea = lax.axis_index("sea")
    index = where_sea * points - halo + jnp.arange(points + 2 * halo, dtype=jnp.int32)
    valid = (index >= 0) & (index < total_points)
    left_k = jnp.where(valid & (index >= 1), kappa_ext[:-1], 0.0)
    right_k = jnp.where(valid & (index < total_points - 1), kappa_ext[1:], 0.0)
    react_v = jnp.where(valid, react_ext, 1.0)
    diag = left_k + right_k + react_v
    return left_k[:, None, None], right_k[:, None, None], diag[:, None, None]


def smooth(source, left_k, right_k, diag, halo):
    weights = omega_table(SWEEPS)
    state = weights[0] * source / diag
    for k in range(1, SWEEPS):
        padded = jnp.pad(state, ((1, 1), (0, 0), (0, 0)))
        applied = diag * state - left_k * padded[:-2] - right_k * padded[2:]
        state = state + weights[k] * (source - applied) / diag
    return state[halo : state.shape[0] - halo]


def dft_tables(steps_all):
    freq_ids = jnp.arange(steps_all, dtype=jnp.int32)
    phase_ids = freq_ids[:, None] * freq_ids[None, :] % steps_all
    angles = phase_ids.astype(jnp.float32) * (2.0 * math.pi / steps_all)
    scale = 1.0 / math.sqrt(steps_all)
    table = jnp.stack([jnp.cos(angles) * scale, -jnp.sin(angles) * scale], axis=1)
    table_high = lax.optimization_barrier(table.astype(jnp.bfloat16))
    table_low = (table - table_high.astype(jnp.float32)).astype(jnp.bfloat16)
    return table_high, table_low


def forward_chunk(prior_part, green, table_high, table_low):
    ways = lax.axis_size("tm")
    piece = lax.all_to_all(prior_part, "tm", split_axis=0, concat_axis=1, tiled=True)
    steps_all = piece.shape[1]
    high = table_high.reshape(ways, steps_all // ways, 2, steps_all)
    low = table_low.reshape(ways, steps_all // ways, 2, steps_all)
    spectrum = jnp.einsum("jfkt,qtc->jfkqc", high, piece, preferred_element_type=jnp.float32)
    spectrum = spectrum + jnp.einsum(
        "jfkt,qtc->jfkqc", low, piece, preferred_element_type=jnp.float32
    )
    spectrum = spectrum.astype(jnp.bfloat16)
    spectra = lax.all_to_all(spectrum, "tm", split_axis=0, concat_axis=0)
    real_s = spectra[:, :, 0]
    imag_s = spectra[:, :, 1]
    mixed = jnp.stack(
        [jnp.stack([real_s, imag_s], axis=2), jnp.stack([-imag_s, real_s], axis=2)], axis=0
    )
    blocks = green.reshape(green.shape[:3] + (ways, green.shape[3] // ways))
    partial = jnp.einsum("fksjq,kjfrqc->fsrc", blocks, mixed, preferred_element_type=jnp.float32)
    summed = lax.psum_scatter(partial.astype(jnp.bfloat16), "sea", scatter_dimension=1, tiled=True)
    return jnp.transpose(summed, (1, 0, 2, 3)).astype(jnp.float32)


def on_device(motion, kappa, react, green):
    halo = SWEEPS - 1
    cols = motion.shape[2]
    width = cols // CHUNKS
    motion_ext, kappa_ext, react_ext = exchange_halo(motion, kappa, react, halo)
    left_k, right_k, diag = extended_coefficients(kappa_ext, react_ext, motion.shape[0], halo)
    table_high, table_low = dft_tables(motion.shape[1] * lax.axis_size("tm"))
    priors = []
    sensors = []
    for c in range(CHUNKS):
        source = motion_ext[:, :, c * width : (c + 1) * width]
        if priors:
            source, _ = lax.optimization_barrier((source, priors[-1]))
        prior_part = smooth(source.astype(jnp.float32), left_k, right_k, diag, halo).astype(jnp.bfloat16)
        priors.append(prior_part)
        sensors.append(forward_chunk(prior_part, green, table_high, table_low))
    return (jnp.concatenate(priors, axis=2), jnp.concatenate(sensors, axis=3))


def solution(mesh):
    in_specs = (P("sea", "tm", None), P("sea"), P("sea"), P("tm", None, None, "sea"))
    out_specs = (P("sea", "tm", None), P("sea", "tm", None, None))
    return jax.shard_map(
        on_device, mesh=mesh, in_specs=in_specs, out_specs=out_specs, check_vma=False
    )
```

```python
import math

import jax
import jax.numpy as jnp
from jax import lax
from jax.sharding import PartitionSpec as P

SWEEPS = 6
CHUNKS = 2


def from_left(block, axis):
    count = lax.axis_size(axis)
    return lax.ppermute(block, axis, [(i, i + 1) for i in range(count - 1)])


def from_right(block, axis):
    count = lax.axis_size(axis)
    return lax.ppermute(block, axis, [(i + 1, i) for i in range(count - 1)])


def omega_table(count):
    return [
        1.0 / (1.05 + 0.95 * math.cos((2 * k + 1) * math.pi / (2 * count))) for k in range(count)
    ]


def exchange_halo(motion, kappa, react, halo):
    points = motion.shape[0]
    shape = (halo,) + motion.shape[1:]
    size = math.prod(shape)
    tail = jnp.concatenate(
        [motion[points - halo :].astype(jnp.float32).reshape(-1), kappa[points - halo - 1 :], react[points - halo :]]
    )
    head = jnp.concatenate(
        [motion[:halo].astype(jnp.float32).reshape(-1), kappa[:halo], react[:halo]]
    )
    before = from_left(tail, "sea")
    after = from_right(head, "sea")
    motion_ext = jnp.concatenate(
        [
            before[:size].reshape(shape).astype(motion.dtype),
            motion,
            after[:size].reshape(shape).astype(motion.dtype),
        ]
    )
    kappa_ext = jnp.concatenate([before[size : size + halo + 1], kappa, after[size : size + halo]])
    react_ext = jnp.concatenate([before[size + halo + 1 :], react, after[size + halo :]])
    return motion_ext, kappa_ext, react_ext


def extended_coefficients(kappa_ext, react_ext, points, halo):
    groups = lax.axis_size("sea")
    total_points = points * groups
    where_sea = lax.axis_index("sea")
    index = where_sea * points - halo + jnp.arange(points + 2 * halo, dtype=jnp.int32)
    valid = (index >= 0) & (index < total_points)
    left_k = jnp.where(valid & (index >= 1), kappa_ext[:-1], 0.0)
    right_k = jnp.where(valid & (index < total_points - 1), kappa_ext[1:], 0.0)
    react_v = jnp.where(valid, react_ext, 1.0)
    diag = left_k + right_k + react_v
    return left_k[:, None, None], right_k[:, None, None], diag[:, None, None]


def smooth(source, left_k, right_k, diag, halo):
    weights = omega_table(SWEEPS)
    state = weights[0] * source / diag
    for k in range(1, SWEEPS):
        padded = jnp.pad(state, ((1, 1), (0, 0), (0, 0)))
        applied = diag * state - left_k * padded[:-2] - right_k * padded[2:]
        state = state + weights[k] * (source - applied) / diag
    return state[halo : state.shape[0] - halo]


def dft_tables(steps_all):
    freq_ids = jnp.arange(steps_all, dtype=jnp.int32)
    phase_ids = freq_ids[:, None] * freq_ids[None, :] % steps_all
    angles = phase_ids.astype(jnp.float32) * (2.0 * math.pi / steps_all)
    scale = 1.0 / math.sqrt(steps_all)
    table = jnp.stack([jnp.cos(angles) * scale, -jnp.sin(angles) * scale], axis=1)
    table_high = lax.optimization_barrier(table.astype(jnp.bfloat16))
    table_low = (table - table_high.astype(jnp.float32)).astype(jnp.bfloat16)
    return table_high, table_low


def forward_chunk(prior_part, green, table_high, table_low):
    ways = lax.axis_size("tm")
    piece = lax.all_to_all(prior_part, "tm", split_axis=0, concat_axis=1, tiled=True)
    steps_all = piece.shape[1]
    high = table_high.reshape(ways, steps_all // ways, 2, steps_all)
    low = table_low.reshape(ways, steps_all // ways, 2, steps_all)
    spectrum = jnp.einsum("jfkt,qtc->jfkqc", high, piece, preferred_element_type=jnp.float32)
    spectrum = spectrum + jnp.einsum(
        "jfkt,qtc->jfkqc", low, piece, preferred_element_type=jnp.float32
    )
    spectrum = spectrum.astype(jnp.bfloat16)
    spectra = lax.all_to_all(spectrum, "tm", split_axis=0, concat_axis=0)
    real_s = spectra[:, :, 0]
    imag_s = spectra[:, :, 1]
    mixed = jnp.stack(
        [jnp.stack([real_s, imag_s], axis=2), jnp.stack([-imag_s, real_s], axis=2)], axis=0
    )
    blocks = green.reshape(green.shape[:3] + (ways, green.shape[3] // ways))
    partial = jnp.einsum("fksjq,kjfrqc->fsrc", blocks, mixed, preferred_element_type=jnp.float32)
    summed = lax.psum_scatter(partial.astype(jnp.bfloat16), "sea", scatter_dimension=1, tiled=True)
    return jnp.transpose(summed, (1, 0, 2, 3)).astype(jnp.float32)


def gathered_tables(blocks, steps_all):
    ways = lax.axis_size("tm")
    where_tm = lax.axis_index("tm").astype(jnp.int32)
    local = steps_all // ways
    freq_ids = where_tm * local + jnp.arange(local, dtype=jnp.int32)
    step_ids = (jnp.stack(blocks)[:, None] * local + jnp.arange(local, dtype=jnp.int32)).reshape(-1)
    phase_ids = freq_ids[:, None] * step_ids[None, :] % steps_all
    angles = phase_ids.astype(jnp.float32) * (2.0 * math.pi / steps_all)
    scale = 1.0 / math.sqrt(steps_all)
    real_w = jnp.cos(angles) * scale
    imag_w = -jnp.sin(angles) * scale
    table = jnp.stack(
        [jnp.stack([real_w, imag_w], axis=1), jnp.stack([-imag_w, real_w], axis=1)], axis=1
    )
    table_high = lax.optimization_barrier(table.astype(jnp.bfloat16))
    table_low = (table - table_high.astype(jnp.float32)).astype(jnp.bfloat16)
    return table_high, table_low


def forward_gathered(prior_part, green):
    where_tm = lax.axis_index("tm").astype(jnp.int32)
    across = lax.ppermute(prior_part, "tm", [(0, 2), (2, 0), (1, 3), (3, 1)])
    mine = jnp.concatenate([prior_part, across], axis=1)
    theirs = lax.ppermute(mine, "tm", [(0, 1), (1, 0), (2, 3), (3, 2)])
    stacked = jnp.concatenate([mine, theirs], axis=1)
    blocks = [where_tm, where_tm ^ 2, where_tm ^ 1, where_tm ^ 3]
    steps_all = prior_part.shape[1] * len(blocks)
    table_high, table_low = gathered_tables(blocks, steps_all)
    mixed = jnp.einsum("fkrt,ptc->fkrpc", table_high, stacked, preferred_element_type=jnp.float32)
    mixed = mixed + jnp.einsum(
        "fkrt,ptc->fkrpc", table_low, stacked, preferred_element_type=jnp.float32
    )
    mixed = mixed.astype(jnp.bfloat16)
    partial = jnp.einsum("fksp,fkrpc->fsrc", green, mixed, preferred_element_type=jnp.float32)
    summed = lax.psum_scatter(partial.astype(jnp.bfloat16), "sea", scatter_dimension=1, tiled=True)
    return jnp.transpose(summed, (1, 0, 2, 3)).astype(jnp.float32)


def on_device(motion, kappa, react, green):
    halo = SWEEPS - 1
    cols = motion.shape[2]
    width = cols // CHUNKS
    motion_ext, kappa_ext, react_ext = exchange_halo(motion, kappa, react, halo)
    left_k, right_k, diag = extended_coefficients(kappa_ext, react_ext, motion.shape[0], halo)
    table_high, table_low = dft_tables(motion.shape[1] * lax.axis_size("tm"))
    priors = []
    sensors = []
    for c in range(CHUNKS):
        source = motion_ext[:, :, c * width : (c + 1) * width]
        if priors:
            source, _ = lax.optimization_barrier((source, priors[-1]))
        prior_part = smooth(source.astype(jnp.float32), left_k, right_k, diag, halo).astype(jnp.bfloat16)
        priors.append(prior_part)
        if lax.axis_size("tm") == 4:
            sensors.append(forward_gathered(prior_part, green))
        else:
            sensors.append(forward_chunk(prior_part, green, table_high, table_low))
    return (jnp.concatenate(priors, axis=2), jnp.concatenate(sensors, axis=3))


def solution(mesh):
    in_specs = (P("sea", "tm", None), P("sea"), P("sea"), P("tm", None, None, "sea"))
    out_specs = (P("sea", "tm", None), P("sea", "tm", None, None))
    return jax.shard_map(
        on_device, mesh=mesh, in_specs=in_specs, out_specs=out_specs, check_vma=False
    )
```

```python
import math

import jax
import jax.numpy as jnp
from jax import lax
from jax.sharding import PartitionSpec as P

SWEEPS = 6
CHUNKS = 2


def from_left(block, axis):
    count = lax.axis_size(axis)
    return lax.ppermute(block, axis, [(i, i + 1) for i in range(count - 1)])


def from_right(block, axis):
    count = lax.axis_size(axis)
    return lax.ppermute(block, axis, [(i + 1, i) for i in range(count - 1)])


def omega_table(count):
    return [
        1.0 / (1.05 + 0.95 * math.cos((2 * k + 1) * math.pi / (2 * count))) for k in range(count)
    ]


def exchange_halo(motion, kappa, react, halo):
    points = motion.shape[0]
    shape = (halo,) + motion.shape[1:]
    size = math.prod(shape)
    tail = jnp.concatenate(
        [motion[points - halo :].astype(jnp.float32).reshape(-1), kappa[points - halo - 1 :], react[points - halo :]]
    )
    head = jnp.concatenate(
        [motion[:halo].astype(jnp.float32).reshape(-1), kappa[:halo], react[:halo]]
    )
    before = from_left(tail, "sea")
    after = from_right(head, "sea")
    motion_ext = jnp.concatenate(
        [
            before[:size].reshape(shape).astype(motion.dtype),
            motion,
            after[:size].reshape(shape).astype(motion.dtype),
        ]
    )
    kappa_ext = jnp.concatenate([before[size : size + halo + 1], kappa, after[size : size + halo]])
    react_ext = jnp.concatenate([before[size + halo + 1 :], react, after[size + halo :]])
    return motion_ext, kappa_ext, react_ext


def extended_coefficients(kappa_ext, react_ext, points, halo):
    groups = lax.axis_size("sea")
    total_points = points * groups
    where_sea = lax.axis_index("sea")
    index = where_sea * points - halo + jnp.arange(points + 2 * halo, dtype=jnp.int32)
    valid = (index >= 0) & (index < total_points)
    left_k = jnp.where(valid & (index >= 1), kappa_ext[:-1], 0.0)
    right_k = jnp.where(valid & (index < total_points - 1), kappa_ext[1:], 0.0)
    react_v = jnp.where(valid, react_ext, 1.0)
    diag = left_k + right_k + react_v
    return left_k[:, None, None], right_k[:, None, None], diag[:, None, None]


def smooth(source, left_k, right_k, diag, halo):
    weights = omega_table(SWEEPS)
    state = weights[0] * source / diag
    for k in range(1, SWEEPS):
        padded = jnp.pad(state, ((1, 1), (0, 0), (0, 0)))
        applied = diag * state - left_k * padded[:-2] - right_k * padded[2:]
        state = state + weights[k] * (source - applied) / diag
    return state[halo : state.shape[0] - halo]


def dft_tables(steps_all):
    freq_ids = jnp.arange(steps_all, dtype=jnp.int32)
    phase_ids = freq_ids[:, None] * freq_ids[None, :] % steps_all
    angles = phase_ids.astype(jnp.float32) * (2.0 * math.pi / steps_all)
    scale = 1.0 / math.sqrt(steps_all)
    table = jnp.stack([jnp.cos(angles) * scale, -jnp.sin(angles) * scale], axis=1)
    table_high = lax.optimization_barrier(table.astype(jnp.bfloat16))
    table_low = (table - table_high.astype(jnp.float32)).astype(jnp.bfloat16)
    return table_high, table_low


def forward_chunk(prior_part, green, table_high, table_low):
    ways = lax.axis_size("tm")
    piece = lax.all_to_all(prior_part, "tm", split_axis=0, concat_axis=1, tiled=True)
    steps_all = piece.shape[1]
    high = table_high.reshape(ways, steps_all // ways, 2, steps_all)
    low = table_low.reshape(ways, steps_all // ways, 2, steps_all)
    spectrum = jnp.einsum("jfkt,qtc->jfkqc", high, piece, preferred_element_type=jnp.float32)
    spectrum = spectrum + jnp.einsum(
        "jfkt,qtc->jfkqc", low, piece, preferred_element_type=jnp.float32
    )
    spectrum = spectrum.astype(jnp.bfloat16)
    spectra = lax.all_to_all(spectrum, "tm", split_axis=0, concat_axis=0)
    real_s = spectra[:, :, 0]
    imag_s = spectra[:, :, 1]
    mixed = jnp.stack(
        [jnp.stack([real_s, imag_s], axis=2), jnp.stack([-imag_s, real_s], axis=2)], axis=0
    )
    blocks = green.reshape(green.shape[:3] + (ways, green.shape[3] // ways))
    partial = jnp.einsum("fksjq,kjfrqc->fsrc", blocks, mixed, preferred_element_type=jnp.float32)
    summed = lax.psum_scatter(partial.astype(jnp.bfloat16), "sea", scatter_dimension=1, tiled=True)
    return jnp.transpose(summed, (1, 0, 2, 3)).astype(jnp.float32)


def gathered_tables(blocks, steps_all):
    ways = lax.axis_size("tm")
    where_tm = lax.axis_index("tm").astype(jnp.int32)
    local = steps_all // ways
    freq_ids = where_tm * local + jnp.arange(local, dtype=jnp.int32)
    step_ids = (jnp.stack(blocks)[:, None] * local + jnp.arange(local, dtype=jnp.int32)).reshape(-1)
    phase_ids = freq_ids[:, None] * step_ids[None, :] % steps_all
    angles = phase_ids.astype(jnp.float32) * (2.0 * math.pi / steps_all)
    scale = 1.0 / math.sqrt(steps_all)
    real_w = jnp.cos(angles) * scale
    imag_w = -jnp.sin(angles) * scale
    table = jnp.stack(
        [jnp.stack([real_w, imag_w], axis=1), jnp.stack([-imag_w, real_w], axis=1)], axis=1
    )
    table_high = lax.optimization_barrier(table.astype(jnp.bfloat16))
    table_low = (table - table_high.astype(jnp.float32)).astype(jnp.bfloat16)
    return table_high, table_low


def gathered_spectrum(prior_part, after=None):
    where_tm = lax.axis_index("tm").astype(jnp.int32)
    across = lax.ppermute(prior_part, "tm", [(0, 2), (2, 0), (1, 3), (3, 1)])
    if after is not None:
        across, _ = lax.optimization_barrier((across, after))
    mine = jnp.concatenate([prior_part, across], axis=1)
    theirs = lax.ppermute(mine, "tm", [(0, 1), (1, 0), (2, 3), (3, 2)])
    stacked = jnp.concatenate([mine, theirs], axis=1)
    blocks = [where_tm, where_tm ^ 2, where_tm ^ 1, where_tm ^ 3]
    steps_all = prior_part.shape[1] * len(blocks)
    table_high, _ = gathered_tables(blocks, steps_all)
    mixed = jnp.einsum("fkrt,ptc->fkrpc", table_high, stacked, preferred_element_type=jnp.float32)
    return mixed.astype(jnp.bfloat16)


def green_product(mixed, green):
    partial = jnp.einsum("fksp,fkrpc->fsrc", green, mixed, preferred_element_type=jnp.float32)
    summed = lax.psum_scatter(partial.astype(jnp.bfloat16), "sea", scatter_dimension=1, tiled=True)
    return jnp.transpose(summed, (1, 0, 2, 3)).astype(jnp.float32)


def on_device(motion, kappa, react, green):
    halo = SWEEPS - 1
    cols = motion.shape[2]
    width = cols // CHUNKS
    motion_ext, kappa_ext, react_ext = exchange_halo(motion, kappa, react, halo)
    left_k, right_k, diag = extended_coefficients(kappa_ext, react_ext, motion.shape[0], halo)
    table_high, table_low = dft_tables(motion.shape[1] * lax.axis_size("tm"))
    priors = []
    spectra = []
    sensors = []
    for c in range(CHUNKS):
        source = motion_ext[:, :, c * width : (c + 1) * width]
        if priors:
            source, _ = lax.optimization_barrier((source, priors[-1]))
        prior_part = smooth(source.astype(jnp.float32), left_k, right_k, diag, halo).astype(jnp.bfloat16)
        priors.append(prior_part)
        if lax.axis_size("tm") == 4:
            mixed = gathered_spectrum(prior_part, spectra[-1] if spectra else None)
            spectra.append(mixed)
            sensors.append(green_product(mixed, green))
        else:
            sensors.append(forward_chunk(prior_part, green, table_high, table_low))
    return (jnp.concatenate(priors, axis=2), jnp.concatenate(sensors, axis=3))


def solution(mesh):
    in_specs = (P("sea", "tm", None), P("sea"), P("sea"), P("tm", None, None, "sea"))
    out_specs = (P("sea", "tm", None), P("sea", "tm", None, None))
    return jax.shard_map(
        on_device, mesh=mesh, in_specs=in_specs, out_specs=out_specs, check_vma=False
    )
```

```python
import math

import jax
import jax.numpy as jnp
from jax import lax
from jax.sharding import PartitionSpec as P

SWEEPS = 6
CHUNKS = 2


def from_left(block, axis):
    count = lax.axis_size(axis)
    return lax.ppermute(block, axis, [(i, i + 1) for i in range(count - 1)])


def from_right(block, axis):
    count = lax.axis_size(axis)
    return lax.ppermute(block, axis, [(i + 1, i) for i in range(count - 1)])


def omega_table(count):
    return [
        1.0 / (1.05 + 0.95 * math.cos((2 * k + 1) * math.pi / (2 * count))) for k in range(count)
    ]


def exchange_halo(motion, kappa, react, halo):
    points = motion.shape[0]
    shape = (halo,) + motion.shape[1:]
    size = math.prod(shape)
    tail = jnp.concatenate(
        [motion[points - halo :].astype(jnp.float32).reshape(-1), kappa[points - halo - 1 :], react[points - halo :]]
    )
    head = jnp.concatenate(
        [motion[:halo].astype(jnp.float32).reshape(-1), kappa[:halo], react[:halo]]
    )
    before = from_left(tail, "sea")
    after = from_right(head, "sea")
    halo_rows = (
        before[:size].reshape(shape).astype(motion.dtype),
        after[:size].reshape(shape).astype(motion.dtype),
    )
    kappa_ext = jnp.concatenate([before[size : size + halo + 1], kappa, after[size : size + halo]])
    react_ext = jnp.concatenate([before[size + halo + 1 :], react, after[size + halo :]])
    return halo_rows, kappa_ext, react_ext


def extended_coefficients(kappa_ext, react_ext, points, halo):
    groups = lax.axis_size("sea")
    total_points = points * groups
    where_sea = lax.axis_index("sea")
    index = where_sea * points - halo + jnp.arange(points + 2 * halo, dtype=jnp.int32)
    valid = (index >= 0) & (index < total_points)
    left_k = jnp.where(valid & (index >= 1), kappa_ext[:-1], 0.0)
    right_k = jnp.where(valid & (index < total_points - 1), kappa_ext[1:], 0.0)
    react_v = jnp.where(valid, react_ext, 1.0)
    diag = left_k + right_k + react_v
    return left_k[:, None, None], right_k[:, None, None], diag[:, None, None]


def smooth(source, left_k, right_k, diag, halo):
    weights = omega_table(SWEEPS)
    state = weights[0] * source / diag
    for k in range(1, SWEEPS):
        padded = jnp.pad(state, ((1, 1), (0, 0), (0, 0)))
        applied = diag * state - left_k * padded[:-2] - right_k * padded[2:]
        state = state + weights[k] * (source - applied) / diag
    return state[halo : state.shape[0] - halo]


def local_coefficients(kappa, react):
    points = kappa.shape[0]
    total_points = points * lax.axis_size("sea")
    index = lax.axis_index("sea") * points + jnp.arange(points, dtype=jnp.int32)
    left_k = jnp.concatenate([jnp.zeros((1,), kappa.dtype), kappa[:-1]])
    right_k = jnp.where(index == total_points - 1, 0.0, kappa)
    diag = left_k + right_k + react
    return left_k[:, None, None], right_k[:, None, None], diag[:, None, None]


def smooth_with_edges(motion, halo_rows, coefficients, local_coefficients_, halo):
    points = motion.shape[0]
    span = 3 * halo + 1
    keep = halo + 1
    interior = smooth(motion.astype(jnp.float32), *local_coefficients_, 0).astype(jnp.bfloat16)
    before, after = halo_rows
    left_src = jnp.concatenate([before, motion[: span - halo]]).astype(jnp.float32)
    right_src = jnp.concatenate([motion[points - span + halo :], after]).astype(jnp.float32)
    left_k, right_k, diag = coefficients
    extent = left_k.shape[0]
    left = smooth(left_src, left_k[:span], right_k[:span], diag[:span], halo)
    right = smooth(
        right_src, left_k[extent - span :], right_k[extent - span :], diag[extent - span :], halo
    )
    interior = lax.dynamic_update_slice_in_dim(interior, left.astype(jnp.bfloat16), 0, 0)
    return lax.dynamic_update_slice_in_dim(
        interior, right.astype(jnp.bfloat16), points - keep, 0
    )


def dft_tables(steps_all):
    freq_ids = jnp.arange(steps_all, dtype=jnp.int32)
    phase_ids = freq_ids[:, None] * freq_ids[None, :] % steps_all
    angles = phase_ids.astype(jnp.float32) * (2.0 * math.pi / steps_all)
    scale = 1.0 / math.sqrt(steps_all)
    table = jnp.stack([jnp.cos(angles) * scale, -jnp.sin(angles) * scale], axis=1)
    table_high = lax.optimization_barrier(table.astype(jnp.bfloat16))
    table_low = (table - table_high.astype(jnp.float32)).astype(jnp.bfloat16)
    return table_high, table_low


def forward_chunk(prior_part, green, table_high, table_low):
    ways = lax.axis_size("tm")
    piece = lax.all_to_all(prior_part, "tm", split_axis=0, concat_axis=1, tiled=True)
    steps_all = piece.shape[1]
    high = table_high.reshape(ways, steps_all // ways, 2, steps_all)
    low = table_low.reshape(ways, steps_all // ways, 2, steps_all)
    spectrum = jnp.einsum("jfkt,qtc->jfkqc", high, piece, preferred_element_type=jnp.float32)
    spectrum = spectrum + jnp.einsum(
        "jfkt,qtc->jfkqc", low, piece, preferred_element_type=jnp.float32
    )
    spectrum = spectrum.astype(jnp.bfloat16)
    spectra = lax.all_to_all(spectrum, "tm", split_axis=0, concat_axis=0)
    real_s = spectra[:, :, 0]
    imag_s = spectra[:, :, 1]
    mixed = jnp.stack(
        [jnp.stack([real_s, imag_s], axis=2), jnp.stack([-imag_s, real_s], axis=2)], axis=0
    )
    blocks = green.reshape(green.shape[:3] + (ways, green.shape[3] // ways))
    partial = jnp.einsum("fksjq,kjfrqc->fsrc", blocks, mixed, preferred_element_type=jnp.float32)
    summed = lax.psum_scatter(partial.astype(jnp.bfloat16), "sea", scatter_dimension=1, tiled=True)
    return jnp.transpose(summed, (1, 0, 2, 3)).astype(jnp.float32)


def gathered_tables(blocks, steps_all):
    ways = lax.axis_size("tm")
    where_tm = lax.axis_index("tm").astype(jnp.int32)
    local = steps_all // ways
    freq_ids = where_tm * local + jnp.arange(local, dtype=jnp.int32)
    step_ids = (jnp.stack(blocks)[:, None] * local + jnp.arange(local, dtype=jnp.int32)).reshape(-1)
    phase_ids = freq_ids[:, None] * step_ids[None, :] % steps_all
    angles = phase_ids.astype(jnp.float32) * (2.0 * math.pi / steps_all)
    scale = 1.0 / math.sqrt(steps_all)
    real_w = jnp.cos(angles) * scale
    imag_w = -jnp.sin(angles) * scale
    table = jnp.stack(
        [jnp.stack([real_w, imag_w], axis=1), jnp.stack([-imag_w, real_w], axis=1)], axis=1
    )
    table_high = lax.optimization_barrier(table.astype(jnp.bfloat16))
    table_low = (table - table_high.astype(jnp.float32)).astype(jnp.bfloat16)
    return table_high, table_low


def gathered_spectrum(prior_part, after=None):
    where_tm = lax.axis_index("tm").astype(jnp.int32)
    across = lax.ppermute(prior_part, "tm", [(0, 2), (2, 0), (1, 3), (3, 1)])
    if after is not None:
        across, _ = lax.optimization_barrier((across, after))
    mine = jnp.concatenate([prior_part, across], axis=1)
    theirs = lax.ppermute(mine, "tm", [(0, 1), (1, 0), (2, 3), (3, 2)])
    stacked = jnp.concatenate([mine, theirs], axis=1)
    blocks = [where_tm, where_tm ^ 2, where_tm ^ 1, where_tm ^ 3]
    steps_all = prior_part.shape[1] * len(blocks)
    table_high, _ = gathered_tables(blocks, steps_all)
    mixed = jnp.einsum("fkrt,ptc->fkrpc", table_high, stacked, preferred_element_type=jnp.float32)
    return mixed.astype(jnp.bfloat16)


def green_product(mixed, green):
    partial = jnp.einsum("fksp,fkrpc->fsrc", green, mixed, preferred_element_type=jnp.float32)
    summed = lax.psum_scatter(partial.astype(jnp.bfloat16), "sea", scatter_dimension=1, tiled=True)
    return jnp.transpose(summed, (1, 0, 2, 3)).astype(jnp.float32)


def on_device(motion, kappa, react, green):
    halo = SWEEPS - 1
    cols = motion.shape[2]
    width = cols // CHUNKS
    halo_rows, kappa_ext, react_ext = exchange_halo(motion, kappa, react, halo)
    coefficients = extended_coefficients(kappa_ext, react_ext, motion.shape[0], halo)
    inner = local_coefficients(kappa, react)
    priors = []
    for c in range(CHUNKS):
        part = slice(c * width, (c + 1) * width)
        source = motion[:, :, part]
        if priors:
            source, _ = lax.optimization_barrier((source, priors[-1]))
        rows = (halo_rows[0][:, :, part], halo_rows[1][:, :, part])
        priors.append(smooth_with_edges(source, rows, coefficients, inner, halo))
    sensors = []
    if lax.axis_size("tm") == 4:
        spectra = []
        for c in range(CHUNKS):
            if c + 1 < CHUNKS:
                hold = (priors[c + 1],) + tuple(spectra[-1:])
            else:
                hold = tuple(spectra[-1:])
            mixed = gathered_spectrum(priors[c], hold if hold else None)
            spectra.append(mixed)
            sensors.append(green_product(mixed, green))
    else:
        table_high, table_low = dft_tables(motion.shape[1] * lax.axis_size("tm"))
        for prior_part in priors:
            sensors.append(forward_chunk(prior_part, green, table_high, table_low))
    return (jnp.concatenate(priors, axis=2), jnp.concatenate(sensors, axis=3))


def solution(mesh):
    in_specs = (P("sea", "tm", None), P("sea"), P("sea"), P("tm", None, None, "sea"))
    out_specs = (P("sea", "tm", None), P("sea", "tm", None, None))
    return jax.shard_map(
        on_device, mesh=mesh, in_specs=in_specs, out_specs=out_specs, check_vma=False
    )
```

```python
import math

import jax
import jax.numpy as jnp
from jax import lax
from jax.sharding import PartitionSpec as P

SWEEPS = 6
CHUNKS = 2


def from_left(block, axis):
    count = lax.axis_size(axis)
    return lax.ppermute(block, axis, [(i, i + 1) for i in range(count - 1)])


def from_right(block, axis):
    count = lax.axis_size(axis)
    return lax.ppermute(block, axis, [(i + 1, i) for i in range(count - 1)])


def omega_table(count):
    return [
        1.0 / (1.05 + 0.95 * math.cos((2 * k + 1) * math.pi / (2 * count))) for k in range(count)
    ]


def exchange_halo(motion, kappa, react, halo):
    points = motion.shape[0]
    shape = (halo,) + motion.shape[1:]
    size = math.prod(shape)
    tail = jnp.concatenate(
        [motion[points - halo :].astype(jnp.float32).reshape(-1), kappa[points - halo - 1 :], react[points - halo :]]
    )
    head = jnp.concatenate(
        [motion[:halo].astype(jnp.float32).reshape(-1), kappa[:halo], react[:halo]]
    )
    before = from_left(tail, "sea")
    after = from_right(head, "sea")
    halo_rows = (
        before[:size].reshape(shape).astype(motion.dtype),
        after[:size].reshape(shape).astype(motion.dtype),
    )
    kappa_ext = jnp.concatenate([before[size : size + halo + 1], kappa, after[size : size + halo]])
    react_ext = jnp.concatenate([before[size + halo + 1 :], react, after[size + halo :]])
    return halo_rows, kappa_ext, react_ext


def extended_coefficients(kappa_ext, react_ext, points, halo):
    groups = lax.axis_size("sea")
    total_points = points * groups
    where_sea = lax.axis_index("sea")
    index = where_sea * points - halo + jnp.arange(points + 2 * halo, dtype=jnp.int32)
    valid = (index >= 0) & (index < total_points)
    left_k = jnp.where(valid & (index >= 1), kappa_ext[:-1], 0.0)
    right_k = jnp.where(valid & (index < total_points - 1), kappa_ext[1:], 0.0)
    react_v = jnp.where(valid, react_ext, 1.0)
    diag = left_k + right_k + react_v
    return left_k[:, None, None], right_k[:, None, None], diag[:, None, None]


def smooth(source, left_k, right_k, diag, halo):
    weights = omega_table(SWEEPS)
    state = weights[0] * source / diag
    for k in range(1, SWEEPS):
        padded = jnp.pad(state, ((1, 1), (0, 0), (0, 0)))
        applied = diag * state - left_k * padded[:-2] - right_k * padded[2:]
        state = state + weights[k] * (source - applied) / diag
    return state[halo : state.shape[0] - halo]


def local_coefficients(kappa, react):
    points = kappa.shape[0]
    total_points = points * lax.axis_size("sea")
    index = lax.axis_index("sea") * points + jnp.arange(points, dtype=jnp.int32)
    left_k = jnp.concatenate([jnp.zeros((1,), kappa.dtype), kappa[:-1]])
    right_k = jnp.where(index == total_points - 1, 0.0, kappa)
    diag = left_k + right_k + react
    return left_k[:, None, None], right_k[:, None, None], diag[:, None, None]


def banded_smooth(motion, coefficients, halo):
    points = motion.shape[0]
    width = 2 * halo + 1
    rows = jnp.arange(points, dtype=jnp.int32)
    lanes = jnp.arange(width, dtype=jnp.int32)
    probe = (rows[:, None] % width == lanes[None, :]).astype(jnp.float32)[:, None, :]
    response = smooth(probe, *coefficients, 0)[:, 0, :]
    padded = jnp.pad(motion, ((halo, halo), (0, 0), (0, 0)))
    total = None
    for offset in range(-halo, halo + 1):
        pick = (rows[:, None] + offset) % width == lanes[None, :]
        band = jnp.sum(jnp.where(pick, response, 0.0), axis=1)[:, None, None]
        term = band * padded[halo + offset : halo + offset + points].astype(jnp.float32)
        total = term if total is None else total + term
    return total


def smooth_with_edges(motion, halo_rows, coefficients, local_coefficients_, halo):
    points = motion.shape[0]
    span = 3 * halo + 1
    keep = halo + 1
    interior = banded_smooth(motion, local_coefficients_, halo).astype(jnp.bfloat16)
    before, after = halo_rows
    left_src = jnp.concatenate([before, motion[: span - halo]]).astype(jnp.float32)
    right_src = jnp.concatenate([motion[points - span + halo :], after]).astype(jnp.float32)
    left_k, right_k, diag = coefficients
    extent = left_k.shape[0]
    left = smooth(left_src, left_k[:span], right_k[:span], diag[:span], halo)
    right = smooth(
        right_src, left_k[extent - span :], right_k[extent - span :], diag[extent - span :], halo
    )
    interior = lax.dynamic_update_slice_in_dim(interior, left.astype(jnp.bfloat16), 0, 0)
    return lax.dynamic_update_slice_in_dim(
        interior, right.astype(jnp.bfloat16), points - keep, 0
    )


def dft_tables(steps_all):
    freq_ids = jnp.arange(steps_all, dtype=jnp.int32)
    phase_ids = freq_ids[:, None] * freq_ids[None, :] % steps_all
    angles = phase_ids.astype(jnp.float32) * (2.0 * math.pi / steps_all)
    scale = 1.0 / math.sqrt(steps_all)
    table = jnp.stack([jnp.cos(angles) * scale, -jnp.sin(angles) * scale], axis=1)
    table_high = lax.optimization_barrier(table.astype(jnp.bfloat16))
    table_low = (table - table_high.astype(jnp.float32)).astype(jnp.bfloat16)
    return table_high, table_low


def forward_chunk(prior_part, green, table_high, table_low):
    ways = lax.axis_size("tm")
    piece = lax.all_to_all(prior_part, "tm", split_axis=0, concat_axis=1, tiled=True)
    steps_all = piece.shape[1]
    high = table_high.reshape(ways, steps_all // ways, 2, steps_all)
    low = table_low.reshape(ways, steps_all // ways, 2, steps_all)
    spectrum = jnp.einsum("jfkt,qtc->jfkqc", high, piece, preferred_element_type=jnp.float32)
    spectrum = spectrum + jnp.einsum(
        "jfkt,qtc->jfkqc", low, piece, preferred_element_type=jnp.float32
    )
    spectrum = spectrum.astype(jnp.bfloat16)
    spectra = lax.all_to_all(spectrum, "tm", split_axis=0, concat_axis=0)
    real_s = spectra[:, :, 0]
    imag_s = spectra[:, :, 1]
    mixed = jnp.stack(
        [jnp.stack([real_s, imag_s], axis=2), jnp.stack([-imag_s, real_s], axis=2)], axis=0
    )
    blocks = green.reshape(green.shape[:3] + (ways, green.shape[3] // ways))
    partial = jnp.einsum("fksjq,kjfrqc->fsrc", blocks, mixed, preferred_element_type=jnp.float32)
    summed = lax.psum_scatter(partial.astype(jnp.bfloat16), "sea", scatter_dimension=1, tiled=True)
    return jnp.transpose(summed, (1, 0, 2, 3)).astype(jnp.float32)


def gathered_tables(blocks, steps_all):
    ways = lax.axis_size("tm")
    where_tm = lax.axis_index("tm").astype(jnp.int32)
    local = steps_all // ways
    freq_ids = where_tm * local + jnp.arange(local, dtype=jnp.int32)
    step_ids = (jnp.stack(blocks)[:, None] * local + jnp.arange(local, dtype=jnp.int32)).reshape(-1)
    phase_ids = freq_ids[:, None] * step_ids[None, :] % steps_all
    angles = phase_ids.astype(jnp.float32) * (2.0 * math.pi / steps_all)
    scale = 1.0 / math.sqrt(steps_all)
    real_w = jnp.cos(angles) * scale
    imag_w = -jnp.sin(angles) * scale
    table = jnp.stack(
        [jnp.stack([real_w, imag_w], axis=1), jnp.stack([-imag_w, real_w], axis=1)], axis=1
    )
    table_high = lax.optimization_barrier(table.astype(jnp.bfloat16))
    table_low = (table - table_high.astype(jnp.float32)).astype(jnp.bfloat16)
    return table_high, table_low


def gathered_spectrum(prior_part, after=None):
    where_tm = lax.axis_index("tm").astype(jnp.int32)
    across = lax.ppermute(prior_part, "tm", [(0, 2), (2, 0), (1, 3), (3, 1)])
    if after is not None:
        across, _ = lax.optimization_barrier((across, after))
    mine = jnp.concatenate([prior_part, across], axis=1)
    theirs = lax.ppermute(mine, "tm", [(0, 1), (1, 0), (2, 3), (3, 2)])
    stacked = jnp.concatenate([mine, theirs], axis=1)
    blocks = [where_tm, where_tm ^ 2, where_tm ^ 1, where_tm ^ 3]
    steps_all = prior_part.shape[1] * len(blocks)
    table_high, _ = gathered_tables(blocks, steps_all)
    mixed = jnp.einsum("fkrt,ptc->fkrpc", table_high, stacked, preferred_element_type=jnp.float32)
    return mixed.astype(jnp.bfloat16)


def green_product(mixed, green):
    partial = jnp.einsum("fksp,fkrpc->fsrc", green, mixed, preferred_element_type=jnp.float32)
    summed = lax.psum_scatter(partial.astype(jnp.bfloat16), "sea", scatter_dimension=1, tiled=True)
    return jnp.transpose(summed, (1, 0, 2, 3)).astype(jnp.float32)


def on_device(motion, kappa, react, green):
    halo = SWEEPS - 1
    cols = motion.shape[2]
    width = cols // CHUNKS
    halo_rows, kappa_ext, react_ext = exchange_halo(motion, kappa, react, halo)
    coefficients = extended_coefficients(kappa_ext, react_ext, motion.shape[0], halo)
    inner = local_coefficients(kappa, react)
    priors = []
    for c in range(CHUNKS):
        part = slice(c * width, (c + 1) * width)
        source = motion[:, :, part]
        if priors:
            source, _ = lax.optimization_barrier((source, priors[-1]))
        rows = (halo_rows[0][:, :, part], halo_rows[1][:, :, part])
        priors.append(smooth_with_edges(source, rows, coefficients, inner, halo))
    sensors = []
    if lax.axis_size("tm") == 4:
        spectra = []
        for c in range(CHUNKS):
            if c + 1 < CHUNKS:
                hold = (priors[c + 1],) + tuple(spectra[-1:])
            else:
                hold = tuple(spectra[-1:])
            mixed = gathered_spectrum(priors[c], hold if hold else None)
            spectra.append(mixed)
            sensors.append(green_product(mixed, green))
    else:
        table_high, table_low = dft_tables(motion.shape[1] * lax.axis_size("tm"))
        for prior_part in priors:
            sensors.append(forward_chunk(prior_part, green, table_high, table_low))
    return (jnp.concatenate(priors, axis=2), jnp.concatenate(sensors, axis=3))


def solution(mesh):
    in_specs = (P("sea", "tm", None), P("sea"), P("sea"), P("tm", None, None, "sea"))
    out_specs = (P("sea", "tm", None), P("sea", "tm", None, None))
    return jax.shard_map(
        on_device, mesh=mesh, in_specs=in_specs, out_specs=out_specs, check_vma=False
    )
```

```python
import math

import jax
import jax.numpy as jnp
from jax import lax
from jax.sharding import PartitionSpec as P

SWEEPS = 6
CHUNKS = 2


def from_left(block, axis):
    count = lax.axis_size(axis)
    return lax.ppermute(block, axis, [(i, i + 1) for i in range(count - 1)])


def from_right(block, axis):
    count = lax.axis_size(axis)
    return lax.ppermute(block, axis, [(i + 1, i) for i in range(count - 1)])


def omega_table(count):
    return [
        1.0 / (1.05 + 0.95 * math.cos((2 * k + 1) * math.pi / (2 * count))) for k in range(count)
    ]


def exchange_halo(motion, kappa, react, halo):
    points = motion.shape[0]
    shape = (halo,) + motion.shape[1:]
    size = math.prod(shape)
    tail = jnp.concatenate(
        [motion[points - halo :].astype(jnp.float32).reshape(-1), kappa[points - halo - 1 :], react[points - halo :]]
    )
    head = jnp.concatenate(
        [motion[:halo].astype(jnp.float32).reshape(-1), kappa[:halo], react[:halo]]
    )
    before = from_left(tail, "sea")
    after = from_right(head, "sea")
    halo_rows = (
        before[:size].reshape(shape).astype(motion.dtype),
        after[:size].reshape(shape).astype(motion.dtype),
    )
    kappa_ext = jnp.concatenate([before[size : size + halo + 1], kappa, after[size : size + halo]])
    react_ext = jnp.concatenate([before[size + halo + 1 :], react, after[size + halo :]])
    return halo_rows, kappa_ext, react_ext


def extended_coefficients(kappa_ext, react_ext, points, halo):
    groups = lax.axis_size("sea")
    total_points = points * groups
    where_sea = lax.axis_index("sea")
    index = where_sea * points - halo + jnp.arange(points + 2 * halo, dtype=jnp.int32)
    valid = (index >= 0) & (index < total_points)
    left_k = jnp.where(valid & (index >= 1), kappa_ext[:-1], 0.0)
    right_k = jnp.where(valid & (index < total_points - 1), kappa_ext[1:], 0.0)
    react_v = jnp.where(valid, react_ext, 1.0)
    diag = left_k + right_k + react_v
    return left_k[:, None, None], right_k[:, None, None], diag[:, None, None]


def smooth(source, left_k, right_k, diag, halo):
    weights = omega_table(SWEEPS)
    state = weights[0] * source / diag
    for k in range(1, SWEEPS):
        padded = jnp.pad(state, ((1, 1), (0, 0), (0, 0)))
        applied = diag * state - left_k * padded[:-2] - right_k * padded[2:]
        state = state + weights[k] * (source - applied) / diag
    return state[halo : state.shape[0] - halo]


def local_coefficients(kappa, react):
    points = kappa.shape[0]
    total_points = points * lax.axis_size("sea")
    index = lax.axis_index("sea") * points + jnp.arange(points, dtype=jnp.int32)
    left_k = jnp.concatenate([jnp.zeros((1,), kappa.dtype), kappa[:-1]])
    right_k = jnp.where(index == total_points - 1, 0.0, kappa)
    diag = left_k + right_k + react
    return left_k[:, None, None], right_k[:, None, None], diag[:, None, None]


def smooth_with_edges(motion, halo_rows, coefficients, local_coefficients_, halo):
    points = motion.shape[0]
    span = 3 * halo + 1
    keep = halo + 1
    interior = smooth(motion.astype(jnp.float32), *local_coefficients_, 0).astype(jnp.bfloat16)
    before, after = halo_rows
    left_src = jnp.concatenate([before, motion[: span - halo]]).astype(jnp.float32)
    right_src = jnp.concatenate([motion[points - span + halo :], after]).astype(jnp.float32)
    left_k, right_k, diag = coefficients
    extent = left_k.shape[0]
    left = smooth(left_src, left_k[:span], right_k[:span], diag[:span], halo)
    right = smooth(
        right_src, left_k[extent - span :], right_k[extent - span :], diag[extent - span :], halo
    )
    interior = lax.dynamic_update_slice_in_dim(interior, left.astype(jnp.bfloat16), 0, 0)
    return lax.dynamic_update_slice_in_dim(
        interior, right.astype(jnp.bfloat16), points - keep, 0
    )


def dft_tables(steps_all):
    freq_ids = jnp.arange(steps_all, dtype=jnp.int32)
    phase_ids = freq_ids[:, None] * freq_ids[None, :] % steps_all
    angles = phase_ids.astype(jnp.float32) * (2.0 * math.pi / steps_all)
    scale = 1.0 / math.sqrt(steps_all)
    table = jnp.stack([jnp.cos(angles) * scale, -jnp.sin(angles) * scale], axis=1)
    table_high = lax.optimization_barrier(table.astype(jnp.bfloat16))
    table_low = (table - table_high.astype(jnp.float32)).astype(jnp.bfloat16)
    return table_high, table_low


def forward_chunk(prior_part, green, table_high, table_low):
    ways = lax.axis_size("tm")
    piece = lax.all_to_all(prior_part, "tm", split_axis=0, concat_axis=1, tiled=True)
    steps_all = piece.shape[1]
    high = table_high.reshape(ways, steps_all // ways, 2, steps_all)
    low = table_low.reshape(ways, steps_all // ways, 2, steps_all)
    spectrum = jnp.einsum("jfkt,qtc->jfkqc", high, piece, preferred_element_type=jnp.float32)
    spectrum = spectrum + jnp.einsum(
        "jfkt,qtc->jfkqc", low, piece, preferred_element_type=jnp.float32
    )
    spectrum = spectrum.astype(jnp.bfloat16)
    spectra = lax.all_to_all(spectrum, "tm", split_axis=0, concat_axis=0)
    real_s = spectra[:, :, 0]
    imag_s = spectra[:, :, 1]
    mixed = jnp.stack(
        [jnp.stack([real_s, imag_s], axis=2), jnp.stack([-imag_s, real_s], axis=2)], axis=0
    )
    blocks = green.reshape(green.shape[:3] + (ways, green.shape[3] // ways))
    partial = jnp.einsum("fksjq,kjfrqc->fsrc", blocks, mixed, preferred_element_type=jnp.float32)
    summed = lax.psum_scatter(partial.astype(jnp.bfloat16), "sea", scatter_dimension=1, tiled=True)
    return jnp.transpose(summed, (1, 0, 2, 3)).astype(jnp.float32)


def gathered_tables(blocks, steps_all):
    ways = lax.axis_size("tm")
    where_tm = lax.axis_index("tm").astype(jnp.int32)
    local = steps_all // ways
    freq_ids = where_tm * local + jnp.arange(local, dtype=jnp.int32)
    step_ids = (jnp.stack(blocks)[:, None] * local + jnp.arange(local, dtype=jnp.int32)).reshape(-1)
    phase_ids = freq_ids[:, None] * step_ids[None, :] % steps_all
    angles = phase_ids.astype(jnp.float32) * (2.0 * math.pi / steps_all)
    scale = 1.0 / math.sqrt(steps_all)
    real_w = jnp.cos(angles) * scale
    imag_w = -jnp.sin(angles) * scale
    table = jnp.stack(
        [jnp.stack([real_w, imag_w], axis=1), jnp.stack([-imag_w, real_w], axis=1)], axis=1
    )
    table_high = lax.optimization_barrier(table.astype(jnp.bfloat16))
    table_low = (table - table_high.astype(jnp.float32)).astype(jnp.bfloat16)
    return table_high, table_low


def gathered_spectrum(prior_part, after=None):
    where_tm = lax.axis_index("tm").astype(jnp.int32)
    across = lax.ppermute(prior_part, "tm", [(0, 2), (2, 0), (1, 3), (3, 1)])
    if after is not None:
        across, _ = lax.optimization_barrier((across, after))
    mine = jnp.concatenate([prior_part, across], axis=1)
    theirs = lax.ppermute(mine, "tm", [(0, 1), (1, 0), (2, 3), (3, 2)])
    stacked = jnp.concatenate([mine, theirs], axis=1)
    blocks = [where_tm, where_tm ^ 2, where_tm ^ 1, where_tm ^ 3]
    steps_all = prior_part.shape[1] * len(blocks)
    table_high, _ = gathered_tables(blocks, steps_all)
    mixed = jnp.einsum("fkrt,ptc->fkrpc", table_high, stacked, preferred_element_type=jnp.float32)
    return mixed.astype(jnp.bfloat16)


def halving_reduce_scatter(x):
    count = lax.axis_size("sea")
    where_sea = lax.axis_index("sea")
    bits = count.bit_length() - 1
    freqs, rows, parts, cols = x.shape
    current = x.reshape((freqs,) + (2,) * bits + (rows // count, parts, cols))
    for bit in range(bits):
        axis = bits - bit
        mine = (where_sea >> bit) & 1
        keep = lax.dynamic_index_in_dim(current, mine, axis, keepdims=False)
        send = lax.dynamic_index_in_dim(current, 1 - mine, axis, keepdims=False)
        got = lax.ppermute(send, "sea", [(i, i ^ (1 << bit)) for i in range(count)])
        current = keep.astype(jnp.float32) + got.astype(jnp.float32)
    return current.reshape(freqs, rows // count, parts, cols)


def green_product(mixed, green):
    partial = jnp.einsum("fksp,fkrpc->fsrc", green, mixed, preferred_element_type=jnp.float32)
    rounded = partial.astype(jnp.bfloat16)
    count = lax.axis_size("sea")
    if count & (count - 1) == 0:
        half = rounded.shape[0] // 2
        offloaded = lax.psum_scatter(rounded[:half], "sea", scatter_dimension=1, tiled=True)
        summed = jnp.concatenate(
            [offloaded.astype(jnp.float32), halving_reduce_scatter(rounded[half:])]
        )
    else:
        summed = lax.psum_scatter(rounded, "sea", scatter_dimension=1, tiled=True)
    return jnp.transpose(summed, (1, 0, 2, 3)).astype(jnp.float32)


def on_device(motion, kappa, react, green):
    halo = SWEEPS - 1
    cols = motion.shape[2]
    width = cols // CHUNKS
    halo_rows, kappa_ext, react_ext = exchange_halo(motion, kappa, react, halo)
    coefficients = extended_coefficients(kappa_ext, react_ext, motion.shape[0], halo)
    inner = local_coefficients(kappa, react)
    priors = []
    for c in range(CHUNKS):
        part = slice(c * width, (c + 1) * width)
        source = motion[:, :, part]
        if priors:
            source, _ = lax.optimization_barrier((source, priors[-1]))
        rows = (halo_rows[0][:, :, part], halo_rows[1][:, :, part])
        priors.append(smooth_with_edges(source, rows, coefficients, inner, halo))
    sensors = []
    if lax.axis_size("tm") == 4:
        spectra = []
        for c in range(CHUNKS):
            if c + 1 < CHUNKS:
                hold = (priors[c + 1],) + tuple(spectra[-1:])
            else:
                hold = tuple(spectra[-1:])
            mixed = gathered_spectrum(priors[c], hold if hold else None)
            spectra.append(mixed)
            sensors.append(green_product(mixed, green))
    else:
        table_high, table_low = dft_tables(motion.shape[1] * lax.axis_size("tm"))
        for prior_part in priors:
            sensors.append(forward_chunk(prior_part, green, table_high, table_low))
    return (jnp.concatenate(priors, axis=2), jnp.concatenate(sensors, axis=3))


def solution(mesh):
    in_specs = (P("sea", "tm", None), P("sea"), P("sea"), P("tm", None, None, "sea"))
    out_specs = (P("sea", "tm", None), P("sea", "tm", None, None))
    return jax.shard_map(
        on_device, mesh=mesh, in_specs=in_specs, out_specs=out_specs, check_vma=False
    )
```

```python
import math

import jax
import jax.numpy as jnp
from jax import lax
from jax.sharding import PartitionSpec as P

SWEEPS = 6
CHUNKS = 2


def from_left(block, axis):
    count = lax.axis_size(axis)
    return lax.ppermute(block, axis, [(i, i + 1) for i in range(count - 1)])


def from_right(block, axis):
    count = lax.axis_size(axis)
    return lax.ppermute(block, axis, [(i + 1, i) for i in range(count - 1)])


def omega_table(count):
    return [
        1.0 / (1.05 + 0.95 * math.cos((2 * k + 1) * math.pi / (2 * count))) for k in range(count)
    ]


def exchange_halo(motion, kappa, react, halo):
    points = motion.shape[0]
    shape = (halo,) + motion.shape[1:]
    size = math.prod(shape)
    tail = jnp.concatenate(
        [motion[points - halo :].astype(jnp.float32).reshape(-1), kappa[points - halo - 1 :], react[points - halo :]]
    )
    head = jnp.concatenate(
        [motion[:halo].astype(jnp.float32).reshape(-1), kappa[:halo], react[:halo]]
    )
    before = from_left(tail, "sea")
    after = from_right(head, "sea")
    halo_rows = (
        before[:size].reshape(shape).astype(motion.dtype),
        after[:size].reshape(shape).astype(motion.dtype),
    )
    kappa_ext = jnp.concatenate([before[size : size + halo + 1], kappa, after[size : size + halo]])
    react_ext = jnp.concatenate([before[size + halo + 1 :], react, after[size + halo :]])
    return halo_rows, kappa_ext, react_ext


def extended_coefficients(kappa_ext, react_ext, points, halo):
    groups = lax.axis_size("sea")
    total_points = points * groups
    where_sea = lax.axis_index("sea")
    index = where_sea * points - halo + jnp.arange(points + 2 * halo, dtype=jnp.int32)
    valid = (index >= 0) & (index < total_points)
    left_k = jnp.where(valid & (index >= 1), kappa_ext[:-1], 0.0)
    right_k = jnp.where(valid & (index < total_points - 1), kappa_ext[1:], 0.0)
    react_v = jnp.where(valid, react_ext, 1.0)
    diag = left_k + right_k + react_v
    return left_k[:, None, None], right_k[:, None, None], diag[:, None, None]


def smooth(source, left_k, right_k, diag, halo):
    weights = omega_table(SWEEPS)
    state = weights[0] * source / diag
    for k in range(1, SWEEPS):
        padded = jnp.pad(state, ((1, 1), (0, 0), (0, 0)))
        applied = diag * state - left_k * padded[:-2] - right_k * padded[2:]
        state = state + weights[k] * (source - applied) / diag
    return state[halo : state.shape[0] - halo]


def local_coefficients(kappa, react):
    points = kappa.shape[0]
    total_points = points * lax.axis_size("sea")
    index = lax.axis_index("sea") * points + jnp.arange(points, dtype=jnp.int32)
    left_k = jnp.concatenate([jnp.zeros((1,), kappa.dtype), kappa[:-1]])
    right_k = jnp.where(index == total_points - 1, 0.0, kappa)
    diag = left_k + right_k + react
    return left_k[:, None, None], right_k[:, None, None], diag[:, None, None]


def smooth_with_edges(motion, halo_rows, coefficients, local_coefficients_, halo):
    points = motion.shape[0]
    span = 3 * halo + 1
    keep = halo + 1
    interior = smooth(motion.astype(jnp.float32), *local_coefficients_, 0).astype(jnp.bfloat16)
    before, after = halo_rows
    left_src = jnp.concatenate([before, motion[: span - halo]]).astype(jnp.float32)
    right_src = jnp.concatenate([motion[points - span + halo :], after]).astype(jnp.float32)
    left_k, right_k, diag = coefficients
    extent = left_k.shape[0]
    left = smooth(left_src, left_k[:span], right_k[:span], diag[:span], halo)
    right = smooth(
        right_src, left_k[extent - span :], right_k[extent - span :], diag[extent - span :], halo
    )
    interior = lax.dynamic_update_slice_in_dim(interior, left.astype(jnp.bfloat16), 0, 0)
    return lax.dynamic_update_slice_in_dim(
        interior, right.astype(jnp.bfloat16), points - keep, 0
    )


def dft_tables(steps_all):
    freq_ids = jnp.arange(steps_all, dtype=jnp.int32)
    phase_ids = freq_ids[:, None] * freq_ids[None, :] % steps_all
    angles = phase_ids.astype(jnp.float32) * (2.0 * math.pi / steps_all)
    scale = 1.0 / math.sqrt(steps_all)
    table = jnp.stack([jnp.cos(angles) * scale, -jnp.sin(angles) * scale], axis=1)
    table_high = lax.optimization_barrier(table.astype(jnp.bfloat16))
    table_low = (table - table_high.astype(jnp.float32)).astype(jnp.bfloat16)
    return table_high, table_low


def forward_chunk(prior_part, green, table_high, table_low):
    ways = lax.axis_size("tm")
    piece = lax.all_to_all(prior_part, "tm", split_axis=0, concat_axis=1, tiled=True)
    steps_all = piece.shape[1]
    high = table_high.reshape(ways, steps_all // ways, 2, steps_all)
    low = table_low.reshape(ways, steps_all // ways, 2, steps_all)
    spectrum = jnp.einsum("jfkt,qtc->jfkqc", high, piece, preferred_element_type=jnp.float32)
    spectrum = spectrum + jnp.einsum(
        "jfkt,qtc->jfkqc", low, piece, preferred_element_type=jnp.float32
    )
    spectrum = spectrum.astype(jnp.bfloat16)
    spectra = lax.all_to_all(spectrum, "tm", split_axis=0, concat_axis=0)
    real_s = spectra[:, :, 0]
    imag_s = spectra[:, :, 1]
    mixed = jnp.stack(
        [jnp.stack([real_s, imag_s], axis=2), jnp.stack([-imag_s, real_s], axis=2)], axis=0
    )
    blocks = green.reshape(green.shape[:3] + (ways, green.shape[3] // ways))
    partial = jnp.einsum("fksjq,kjfrqc->fsrc", blocks, mixed, preferred_element_type=jnp.float32)
    summed = lax.psum_scatter(partial.astype(jnp.bfloat16), "sea", scatter_dimension=1, tiled=True)
    return jnp.transpose(summed, (1, 0, 2, 3)).astype(jnp.float32)


def gathered_tables(blocks, steps_all):
    ways = lax.axis_size("tm")
    where_tm = lax.axis_index("tm").astype(jnp.int32)
    local = steps_all // ways
    freq_ids = where_tm * local + jnp.arange(local, dtype=jnp.int32)
    step_ids = (jnp.stack(blocks)[:, None] * local + jnp.arange(local, dtype=jnp.int32)).reshape(-1)
    phase_ids = freq_ids[:, None] * step_ids[None, :] % steps_all
    angles = phase_ids.astype(jnp.float32) * (2.0 * math.pi / steps_all)
    scale = 1.0 / math.sqrt(steps_all)
    real_w = jnp.cos(angles) * scale
    imag_w = -jnp.sin(angles) * scale
    table = jnp.stack(
        [jnp.stack([real_w, imag_w], axis=1), jnp.stack([-imag_w, real_w], axis=1)], axis=1
    )
    table_high = lax.optimization_barrier(table.astype(jnp.bfloat16))
    table_low = (table - table_high.astype(jnp.float32)).astype(jnp.bfloat16)
    return table_high, table_low


def gathered_spectrum(prior_part, after=None):
    where_tm = lax.axis_index("tm").astype(jnp.int32)
    cross_pairs = [(0, 2), (2, 0), (1, 3), (3, 1)]
    chip_pairs = [(0, 1), (1, 0), (2, 3), (3, 2)]
    partner = lax.ppermute(prior_part, "tm", chip_pairs)
    across = lax.ppermute(prior_part, "tm", cross_pairs)
    if after is not None:
        across, _ = lax.optimization_barrier((across, after))
    partner_across = lax.ppermute(across, "tm", chip_pairs)
    early = jnp.concatenate([prior_part, partner], axis=1)
    late = jnp.concatenate([across, partner_across], axis=1)
    blocks = [where_tm, where_tm ^ 1, where_tm ^ 2, where_tm ^ 3]
    steps_all = prior_part.shape[1] * len(blocks)
    table_high, _ = gathered_tables(blocks, steps_all)
    half = steps_all // 2
    mixed = jnp.einsum(
        "fkrt,ptc->fkrpc", table_high[..., :half], early, preferred_element_type=jnp.float32
    )
    mixed = mixed + jnp.einsum(
        "fkrt,ptc->fkrpc", table_high[..., half:], late, preferred_element_type=jnp.float32
    )
    return mixed.astype(jnp.bfloat16)


def green_product(mixed, green):
    partial = jnp.einsum("fksp,fkrpc->fsrc", green, mixed, preferred_element_type=jnp.float32)
    summed = lax.psum_scatter(partial.astype(jnp.bfloat16), "sea", scatter_dimension=1, tiled=True)
    return jnp.transpose(summed, (1, 0, 2, 3)).astype(jnp.float32)


def on_device(motion, kappa, react, green):
    halo = SWEEPS - 1
    cols = motion.shape[2]
    width = cols // CHUNKS
    halo_rows, kappa_ext, react_ext = exchange_halo(motion, kappa, react, halo)
    coefficients = extended_coefficients(kappa_ext, react_ext, motion.shape[0], halo)
    inner = local_coefficients(kappa, react)
    priors = []
    for c in range(CHUNKS):
        part = slice(c * width, (c + 1) * width)
        source = motion[:, :, part]
        if priors:
            source, _ = lax.optimization_barrier((source, priors[-1]))
        rows = (halo_rows[0][:, :, part], halo_rows[1][:, :, part])
        priors.append(smooth_with_edges(source, rows, coefficients, inner, halo))
    sensors = []
    if lax.axis_size("tm") == 4:
        spectra = []
        for c in range(CHUNKS):
            if c + 1 < CHUNKS:
                hold = (priors[c + 1],) + tuple(spectra[-1:])
            else:
                hold = tuple(spectra[-1:])
            mixed = gathered_spectrum(priors[c], hold if hold else None)
            spectra.append(mixed)
            sensors.append(green_product(mixed, green))
    else:
        table_high, table_low = dft_tables(motion.shape[1] * lax.axis_size("tm"))
        for prior_part in priors:
            sensors.append(forward_chunk(prior_part, green, table_high, table_low))
    return (jnp.concatenate(priors, axis=2), jnp.concatenate(sensors, axis=3))


def solution(mesh):
    in_specs = (P("sea", "tm", None), P("sea"), P("sea"), P("tm", None, None, "sea"))
    out_specs = (P("sea", "tm", None), P("sea", "tm", None, None))
    return jax.shard_map(
        on_device, mesh=mesh, in_specs=in_specs, out_specs=out_specs, check_vma=False
    )
```

```python
import math

import jax
import jax.numpy as jnp
from jax import lax
from jax.sharding import PartitionSpec as P

SWEEPS = 6
CHUNKS = 2


def from_left(block, axis):
    count = lax.axis_size(axis)
    return lax.ppermute(block, axis, [(i, i + 1) for i in range(count - 1)])


def from_right(block, axis):
    count = lax.axis_size(axis)
    return lax.ppermute(block, axis, [(i + 1, i) for i in range(count - 1)])


def omega_table(count):
    return [
        1.0 / (1.05 + 0.95 * math.cos((2 * k + 1) * math.pi / (2 * count))) for k in range(count)
    ]


def exchange_halo(motion, kappa, react, halo):
    points = motion.shape[0]
    shape = (halo,) + motion.shape[1:]
    size = math.prod(shape)
    tail = jnp.concatenate(
        [motion[points - halo :].astype(jnp.float32).reshape(-1), kappa[points - halo - 1 :], react[points - halo :]]
    )
    head = jnp.concatenate(
        [motion[:halo].astype(jnp.float32).reshape(-1), kappa[:halo], react[:halo]]
    )
    before = from_left(tail, "sea")
    after = from_right(head, "sea")
    halo_rows = (
        before[:size].reshape(shape).astype(motion.dtype),
        after[:size].reshape(shape).astype(motion.dtype),
    )
    kappa_ext = jnp.concatenate([before[size : size + halo + 1], kappa, after[size : size + halo]])
    react_ext = jnp.concatenate([before[size + halo + 1 :], react, after[size + halo :]])
    return halo_rows, kappa_ext, react_ext


def extended_coefficients(kappa_ext, react_ext, points, halo):
    groups = lax.axis_size("sea")
    total_points = points * groups
    where_sea = lax.axis_index("sea")
    index = where_sea * points - halo + jnp.arange(points + 2 * halo, dtype=jnp.int32)
    valid = (index >= 0) & (index < total_points)
    left_k = jnp.where(valid & (index >= 1), kappa_ext[:-1], 0.0)
    right_k = jnp.where(valid & (index < total_points - 1), kappa_ext[1:], 0.0)
    react_v = jnp.where(valid, react_ext, 1.0)
    diag = left_k + right_k + react_v
    return left_k[:, None, None], right_k[:, None, None], diag[:, None, None]


def smooth(source, left_k, right_k, diag, halo):
    weights = omega_table(SWEEPS)
    state = weights[0] * source / diag
    for k in range(1, SWEEPS):
        padded = jnp.pad(state, ((1, 1), (0, 0), (0, 0)))
        applied = diag * state - left_k * padded[:-2] - right_k * padded[2:]
        state = state + weights[k] * (source - applied) / diag
    return state[halo : state.shape[0] - halo]


def local_coefficients(kappa, react):
    points = kappa.shape[0]
    total_points = points * lax.axis_size("sea")
    index = lax.axis_index("sea") * points + jnp.arange(points, dtype=jnp.int32)
    left_k = jnp.concatenate([jnp.zeros((1,), kappa.dtype), kappa[:-1]])
    right_k = jnp.where(index == total_points - 1, 0.0, kappa)
    diag = left_k + right_k + react
    return left_k[:, None, None], right_k[:, None, None], diag[:, None, None]


def smooth_with_edges(motion, halo_rows, coefficients, local_coefficients_, halo):
    points = motion.shape[0]
    span = 3 * halo + 1
    keep = halo + 1
    interior = smooth(motion.astype(jnp.float32), *local_coefficients_, 0).astype(jnp.bfloat16)
    before, after = halo_rows
    left_src = jnp.concatenate([before, motion[: span - halo]]).astype(jnp.float32)
    right_src = jnp.concatenate([motion[points - span + halo :], after]).astype(jnp.float32)
    left_k, right_k, diag = coefficients
    extent = left_k.shape[0]
    left = smooth(left_src, left_k[:span], right_k[:span], diag[:span], halo)
    right = smooth(
        right_src, left_k[extent - span :], right_k[extent - span :], diag[extent - span :], halo
    )
    interior = lax.dynamic_update_slice_in_dim(interior, left.astype(jnp.bfloat16), 0, 0)
    return lax.dynamic_update_slice_in_dim(
        interior, right.astype(jnp.bfloat16), points - keep, 0
    )


def dft_tables(steps_all):
    freq_ids = jnp.arange(steps_all, dtype=jnp.int32)
    phase_ids = freq_ids[:, None] * freq_ids[None, :] % steps_all
    angles = phase_ids.astype(jnp.float32) * (2.0 * math.pi / steps_all)
    scale = 1.0 / math.sqrt(steps_all)
    table = jnp.stack([jnp.cos(angles) * scale, -jnp.sin(angles) * scale], axis=1)
    table_high = lax.optimization_barrier(table.astype(jnp.bfloat16))
    table_low = (table - table_high.astype(jnp.float32)).astype(jnp.bfloat16)
    return table_high, table_low


def forward_chunk(prior_part, green, table_high, table_low):
    ways = lax.axis_size("tm")
    piece = lax.all_to_all(prior_part, "tm", split_axis=0, concat_axis=1, tiled=True)
    steps_all = piece.shape[1]
    high = table_high.reshape(ways, steps_all // ways, 2, steps_all)
    low = table_low.reshape(ways, steps_all // ways, 2, steps_all)
    spectrum = jnp.einsum("jfkt,qtc->jfkqc", high, piece, preferred_element_type=jnp.float32)
    spectrum = spectrum + jnp.einsum(
        "jfkt,qtc->jfkqc", low, piece, preferred_element_type=jnp.float32
    )
    spectrum = spectrum.astype(jnp.bfloat16)
    spectra = lax.all_to_all(spectrum, "tm", split_axis=0, concat_axis=0)
    real_s = spectra[:, :, 0]
    imag_s = spectra[:, :, 1]
    mixed = jnp.stack(
        [jnp.stack([real_s, imag_s], axis=2), jnp.stack([-imag_s, real_s], axis=2)], axis=0
    )
    blocks = green.reshape(green.shape[:3] + (ways, green.shape[3] // ways))
    partial = jnp.einsum("fksjq,kjfrqc->fsrc", blocks, mixed, preferred_element_type=jnp.float32)
    summed = lax.psum_scatter(partial.astype(jnp.bfloat16), "sea", scatter_dimension=1, tiled=True)
    return jnp.transpose(summed, (1, 0, 2, 3)).astype(jnp.float32)


def gathered_tables(blocks, steps_all):
    ways = lax.axis_size("tm")
    where_tm = lax.axis_index("tm").astype(jnp.int32)
    local = steps_all // ways
    freq_ids = where_tm * local + jnp.arange(local, dtype=jnp.int32)
    step_ids = (jnp.stack(blocks)[:, None] * local + jnp.arange(local, dtype=jnp.int32)).reshape(-1)
    phase_ids = freq_ids[:, None] * step_ids[None, :] % steps_all
    angles = phase_ids.astype(jnp.float32) * (2.0 * math.pi / steps_all)
    scale = 1.0 / math.sqrt(steps_all)
    real_w = jnp.cos(angles) * scale
    imag_w = -jnp.sin(angles) * scale
    table = jnp.stack(
        [jnp.stack([real_w, imag_w], axis=1), jnp.stack([-imag_w, real_w], axis=1)], axis=1
    )
    table_high = lax.optimization_barrier(table.astype(jnp.bfloat16))
    table_low = (table - table_high.astype(jnp.float32)).astype(jnp.bfloat16)
    return table_high, table_low


def gathered_spectrum(prior_part, after=None):
    where_tm = lax.axis_index("tm").astype(jnp.int32)
    chip_pairs = [(0, 1), (1, 0), (2, 3), (3, 2)]
    across = lax.ppermute(prior_part, "tm", [(0, 2), (2, 0), (1, 3), (3, 1)])
    partner = lax.ppermute(prior_part, "tm", chip_pairs)
    if after is not None:
        across, _ = lax.optimization_barrier((across, after))
    partner_across = lax.ppermute(across, "tm", chip_pairs)
    stacked = jnp.concatenate([prior_part, across, partner, partner_across], axis=1)
    blocks = [where_tm, where_tm ^ 2, where_tm ^ 1, where_tm ^ 3]
    steps_all = prior_part.shape[1] * len(blocks)
    table_high, _ = gathered_tables(blocks, steps_all)
    mixed = jnp.einsum("fkrt,ptc->fkrpc", table_high, stacked, preferred_element_type=jnp.float32)
    return mixed.astype(jnp.bfloat16)


def green_product(mixed, green):
    partial = jnp.einsum("fksp,fkrpc->fsrc", green, mixed, preferred_element_type=jnp.float32)
    summed = lax.psum_scatter(partial.astype(jnp.bfloat16), "sea", scatter_dimension=1, tiled=True)
    return jnp.transpose(summed, (1, 0, 2, 3)).astype(jnp.float32)


def on_device(motion, kappa, react, green):
    halo = SWEEPS - 1
    cols = motion.shape[2]
    width = cols // CHUNKS
    halo_rows, kappa_ext, react_ext = exchange_halo(motion, kappa, react, halo)
    coefficients = extended_coefficients(kappa_ext, react_ext, motion.shape[0], halo)
    inner = local_coefficients(kappa, react)
    priors = []
    for c in range(CHUNKS):
        part = slice(c * width, (c + 1) * width)
        source = motion[:, :, part]
        if priors:
            source, _ = lax.optimization_barrier((source, priors[-1]))
        rows = (halo_rows[0][:, :, part], halo_rows[1][:, :, part])
        priors.append(smooth_with_edges(source, rows, coefficients, inner, halo))
    sensors = []
    if lax.axis_size("tm") == 4:
        spectra = []
        for c in range(CHUNKS):
            if c + 1 < CHUNKS:
                hold = (priors[c + 1],) + tuple(spectra[-1:])
            else:
                hold = tuple(spectra[-1:])
            mixed = gathered_spectrum(priors[c], hold if hold else None)
            spectra.append(mixed)
            sensors.append(green_product(mixed, green))
    else:
        table_high, table_low = dft_tables(motion.shape[1] * lax.axis_size("tm"))
        for prior_part in priors:
            sensors.append(forward_chunk(prior_part, green, table_high, table_low))
    return (jnp.concatenate(priors, axis=2), jnp.concatenate(sensors, axis=3))


def solution(mesh):
    in_specs = (P("sea", "tm", None), P("sea"), P("sea"), P("tm", None, None, "sea"))
    out_specs = (P("sea", "tm", None), P("sea", "tm", None, None))
    return jax.shard_map(
        on_device, mesh=mesh, in_specs=in_specs, out_specs=out_specs, check_vma=False
    )
```

```python
import math

import jax
import jax.numpy as jnp
from jax import lax
from jax.sharding import PartitionSpec as P

SWEEPS = 6
CHUNKS = 2


def from_left(block, axis):
    count = lax.axis_size(axis)
    return lax.ppermute(block, axis, [(i, i + 1) for i in range(count - 1)])


def from_right(block, axis):
    count = lax.axis_size(axis)
    return lax.ppermute(block, axis, [(i + 1, i) for i in range(count - 1)])


def omega_table(count):
    return [
        1.0 / (1.05 + 0.95 * math.cos((2 * k + 1) * math.pi / (2 * count))) for k in range(count)
    ]


def exchange_halo(motion, kappa, react, halo):
    points = motion.shape[0]
    shape = (halo,) + motion.shape[1:]
    size = math.prod(shape)
    tail = jnp.concatenate(
        [motion[points - halo :].astype(jnp.float32).reshape(-1), kappa[points - halo - 1 :], react[points - halo :]]
    )
    head = jnp.concatenate(
        [motion[:halo].astype(jnp.float32).reshape(-1), kappa[:halo], react[:halo]]
    )
    before = from_left(tail, "sea")
    after = from_right(head, "sea")
    halo_rows = (
        before[:size].reshape(shape).astype(motion.dtype),
        after[:size].reshape(shape).astype(motion.dtype),
    )
    kappa_ext = jnp.concatenate([before[size : size + halo + 1], kappa, after[size : size + halo]])
    react_ext = jnp.concatenate([before[size + halo + 1 :], react, after[size + halo :]])
    return halo_rows, kappa_ext, react_ext


def extended_coefficients(kappa_ext, react_ext, points, halo):
    groups = lax.axis_size("sea")
    total_points = points * groups
    where_sea = lax.axis_index("sea")
    index = where_sea * points - halo + jnp.arange(points + 2 * halo, dtype=jnp.int32)
    valid = (index >= 0) & (index < total_points)
    left_k = jnp.where(valid & (index >= 1), kappa_ext[:-1], 0.0)
    right_k = jnp.where(valid & (index < total_points - 1), kappa_ext[1:], 0.0)
    react_v = jnp.where(valid, react_ext, 1.0)
    diag = left_k + right_k + react_v
    return left_k[:, None, None], right_k[:, None, None], diag[:, None, None]


def smooth(source, left_k, right_k, diag, halo):
    weights = omega_table(SWEEPS)
    state = weights[0] * source / diag
    for k in range(1, SWEEPS):
        padded = jnp.pad(state, ((1, 1), (0, 0), (0, 0)))
        applied = diag * state - left_k * padded[:-2] - right_k * padded[2:]
        state = state + weights[k] * (source - applied) / diag
    return state[halo : state.shape[0] - halo]


def local_coefficients(kappa, react):
    points = kappa.shape[0]
    total_points = points * lax.axis_size("sea")
    index = lax.axis_index("sea") * points + jnp.arange(points, dtype=jnp.int32)
    left_k = jnp.concatenate([jnp.zeros((1,), kappa.dtype), kappa[:-1]])
    right_k = jnp.where(index == total_points - 1, 0.0, kappa)
    diag = left_k + right_k + react
    return left_k[:, None, None], right_k[:, None, None], diag[:, None, None]


def banded_smooth(motion, coefficients, halo):
    points = motion.shape[0]
    width = 2 * halo + 1
    rows = jnp.arange(points, dtype=jnp.int32)
    lanes = jnp.arange(width, dtype=jnp.int32)
    probe = (rows[:, None] % width == lanes[None, :]).astype(jnp.float32)[:, None, :]
    response = smooth(probe, *coefficients, 0)[:, 0, :]
    padded = jnp.pad(motion, ((halo, halo), (0, 0), (0, 0)))
    total = None
    for offset in range(-halo, halo + 1):
        pick = (rows[:, None] + offset) % width == lanes[None, :]
        band = jnp.sum(jnp.where(pick, response, 0.0), axis=1)[:, None, None]
        term = band * padded[halo + offset : halo + offset + points].astype(jnp.float32)
        total = term if total is None else total + term
    return total


def smooth_with_edges(motion, halo_rows, coefficients, local_coefficients_, halo, banded=False):
    points = motion.shape[0]
    span = 3 * halo + 1
    keep = halo + 1
    if banded:
        interior = banded_smooth(motion, local_coefficients_, halo).astype(jnp.bfloat16)
    else:
        interior = smooth(motion.astype(jnp.float32), *local_coefficients_, 0).astype(jnp.bfloat16)
    before, after = halo_rows
    left_src = jnp.concatenate([before, motion[: span - halo]]).astype(jnp.float32)
    right_src = jnp.concatenate([motion[points - span + halo :], after]).astype(jnp.float32)
    left_k, right_k, diag = coefficients
    extent = left_k.shape[0]
    left = smooth(left_src, left_k[:span], right_k[:span], diag[:span], halo)
    right = smooth(
        right_src, left_k[extent - span :], right_k[extent - span :], diag[extent - span :], halo
    )
    interior = lax.dynamic_update_slice_in_dim(interior, left.astype(jnp.bfloat16), 0, 0)
    return lax.dynamic_update_slice_in_dim(
        interior, right.astype(jnp.bfloat16), points - keep, 0
    )


def dft_tables(steps_all):
    freq_ids = jnp.arange(steps_all, dtype=jnp.int32)
    phase_ids = freq_ids[:, None] * freq_ids[None, :] % steps_all
    angles = phase_ids.astype(jnp.float32) * (2.0 * math.pi / steps_all)
    scale = 1.0 / math.sqrt(steps_all)
    table = jnp.stack([jnp.cos(angles) * scale, -jnp.sin(angles) * scale], axis=1)
    table_high = lax.optimization_barrier(table.astype(jnp.bfloat16))
    table_low = (table - table_high.astype(jnp.float32)).astype(jnp.bfloat16)
    return table_high, table_low


def forward_chunk(prior_part, green, table_high, table_low):
    ways = lax.axis_size("tm")
    piece = lax.all_to_all(prior_part, "tm", split_axis=0, concat_axis=1, tiled=True)
    steps_all = piece.shape[1]
    high = table_high.reshape(ways, steps_all // ways, 2, steps_all)
    low = table_low.reshape(ways, steps_all // ways, 2, steps_all)
    spectrum = jnp.einsum("jfkt,qtc->jfkqc", high, piece, preferred_element_type=jnp.float32)
    spectrum = spectrum + jnp.einsum(
        "jfkt,qtc->jfkqc", low, piece, preferred_element_type=jnp.float32
    )
    spectrum = spectrum.astype(jnp.bfloat16)
    spectra = lax.all_to_all(spectrum, "tm", split_axis=0, concat_axis=0)
    real_s = spectra[:, :, 0]
    imag_s = spectra[:, :, 1]
    mixed = jnp.stack(
        [jnp.stack([real_s, imag_s], axis=2), jnp.stack([-imag_s, real_s], axis=2)], axis=0
    )
    blocks = green.reshape(green.shape[:3] + (ways, green.shape[3] // ways))
    partial = jnp.einsum("fksjq,kjfrqc->fsrc", blocks, mixed, preferred_element_type=jnp.float32)
    summed = lax.psum_scatter(partial.astype(jnp.bfloat16), "sea", scatter_dimension=1, tiled=True)
    return jnp.transpose(summed, (1, 0, 2, 3)).astype(jnp.float32)


def gathered_tables(blocks, steps_all):
    ways = lax.axis_size("tm")
    where_tm = lax.axis_index("tm").astype(jnp.int32)
    local = steps_all // ways
    freq_ids = where_tm * local + jnp.arange(local, dtype=jnp.int32)
    step_ids = (jnp.stack(blocks)[:, None] * local + jnp.arange(local, dtype=jnp.int32)).reshape(-1)
    phase_ids = freq_ids[:, None] * step_ids[None, :] % steps_all
    angles = phase_ids.astype(jnp.float32) * (2.0 * math.pi / steps_all)
    scale = 1.0 / math.sqrt(steps_all)
    real_w = jnp.cos(angles) * scale
    imag_w = -jnp.sin(angles) * scale
    table = jnp.stack(
        [jnp.stack([real_w, imag_w], axis=1), jnp.stack([-imag_w, real_w], axis=1)], axis=1
    )
    table_high = lax.optimization_barrier(table.astype(jnp.bfloat16))
    table_low = (table - table_high.astype(jnp.float32)).astype(jnp.bfloat16)
    return table_high, table_low


def gathered_spectrum(prior_part, after=None):
    where_tm = lax.axis_index("tm").astype(jnp.int32)
    chip_pairs = [(0, 1), (1, 0), (2, 3), (3, 2)]
    across = lax.ppermute(prior_part, "tm", [(0, 2), (2, 0), (1, 3), (3, 1)])
    partner = lax.ppermute(prior_part, "tm", chip_pairs)
    if after is not None:
        across, _ = lax.optimization_barrier((across, after))
    partner_across = lax.ppermute(across, "tm", chip_pairs)
    stacked = jnp.concatenate([prior_part, across, partner, partner_across], axis=1)
    blocks = [where_tm, where_tm ^ 2, where_tm ^ 1, where_tm ^ 3]
    steps_all = prior_part.shape[1] * len(blocks)
    table_high, _ = gathered_tables(blocks, steps_all)
    mixed = jnp.einsum("fkrt,ptc->fkrpc", table_high, stacked, preferred_element_type=jnp.float32)
    return mixed.astype(jnp.bfloat16)


def green_product(mixed, green):
    partial = jnp.einsum("fksp,fkrpc->fsrc", green, mixed, preferred_element_type=jnp.float32)
    summed = lax.psum_scatter(partial.astype(jnp.bfloat16), "sea", scatter_dimension=1, tiled=True)
    return jnp.transpose(summed, (1, 0, 2, 3)).astype(jnp.float32)


def on_device(motion, kappa, react, green):
    halo = SWEEPS - 1
    cols = motion.shape[2]
    width = cols // CHUNKS
    halo_rows, kappa_ext, react_ext = exchange_halo(motion, kappa, react, halo)
    coefficients = extended_coefficients(kappa_ext, react_ext, motion.shape[0], halo)
    inner = local_coefficients(kappa, react)
    priors = []
    for c in range(CHUNKS):
        part = slice(c * width, (c + 1) * width)
        source = motion[:, :, part]
        if priors:
            source, _ = lax.optimization_barrier((source, priors[-1]))
        rows = (halo_rows[0][:, :, part], halo_rows[1][:, :, part])
        priors.append(smooth_with_edges(source, rows, coefficients, inner, halo, c == 0))
    sensors = []
    if lax.axis_size("tm") == 4:
        spectra = []
        for c in range(CHUNKS):
            if c + 1 < CHUNKS:
                hold = (priors[c + 1],) + tuple(spectra[-1:])
            else:
                hold = tuple(spectra[-1:])
            mixed = gathered_spectrum(priors[c], hold if hold else None)
            spectra.append(mixed)
            sensors.append(green_product(mixed, green))
    else:
        table_high, table_low = dft_tables(motion.shape[1] * lax.axis_size("tm"))
        for prior_part in priors:
            sensors.append(forward_chunk(prior_part, green, table_high, table_low))
    return (jnp.concatenate(priors, axis=2), jnp.concatenate(sensors, axis=3))


def solution(mesh):
    in_specs = (P("sea", "tm", None), P("sea"), P("sea"), P("tm", None, None, "sea"))
    out_specs = (P("sea", "tm", None), P("sea", "tm", None, None))
    return jax.shard_map(
        on_device, mesh=mesh, in_specs=in_specs, out_specs=out_specs, check_vma=False
    )
```

```python
import math

import jax
import jax.numpy as jnp
from jax import lax
from jax.sharding import PartitionSpec as P

SWEEPS = 6
CHUNKS = 2


def from_left(block, axis):
    count = lax.axis_size(axis)
    return lax.ppermute(block, axis, [(i, i + 1) for i in range(count - 1)])


def from_right(block, axis):
    count = lax.axis_size(axis)
    return lax.ppermute(block, axis, [(i + 1, i) for i in range(count - 1)])


def omega_table(count):
    return [
        1.0 / (1.05 + 0.95 * math.cos((2 * k + 1) * math.pi / (2 * count))) for k in range(count)
    ]


def exchange_halo(motion, kappa, react, halo):
    points = motion.shape[0]
    shape = (halo,) + motion.shape[1:]
    size = math.prod(shape)
    tail = jnp.concatenate(
        [motion[points - halo :].astype(jnp.float32).reshape(-1), kappa[points - halo - 1 :], react[points - halo :]]
    )
    head = jnp.concatenate(
        [motion[:halo].astype(jnp.float32).reshape(-1), kappa[:halo], react[:halo]]
    )
    before = from_left(tail, "sea")
    after = from_right(head, "sea")
    halo_rows = (
        before[:size].reshape(shape).astype(motion.dtype),
        after[:size].reshape(shape).astype(motion.dtype),
    )
    kappa_ext = jnp.concatenate([before[size : size + halo + 1], kappa, after[size : size + halo]])
    react_ext = jnp.concatenate([before[size + halo + 1 :], react, after[size + halo :]])
    return halo_rows, kappa_ext, react_ext


def extended_coefficients(kappa_ext, react_ext, points, halo):
    groups = lax.axis_size("sea")
    total_points = points * groups
    where_sea = lax.axis_index("sea")
    index = where_sea * points - halo + jnp.arange(points + 2 * halo, dtype=jnp.int32)
    valid = (index >= 0) & (index < total_points)
    left_k = jnp.where(valid & (index >= 1), kappa_ext[:-1], 0.0)
    right_k = jnp.where(valid & (index < total_points - 1), kappa_ext[1:], 0.0)
    react_v = jnp.where(valid, react_ext, 1.0)
    diag = left_k + right_k + react_v
    return left_k[:, None, None], right_k[:, None, None], diag[:, None, None]


def smooth(source, left_k, right_k, diag, halo):
    weights = omega_table(SWEEPS)
    state = weights[0] * source / diag
    for k in range(1, SWEEPS):
        padded = jnp.pad(state, ((1, 1), (0, 0), (0, 0)))
        applied = diag * state - left_k * padded[:-2] - right_k * padded[2:]
        state = state + weights[k] * (source - applied) / diag
    return state[halo : state.shape[0] - halo]


def local_coefficients(kappa, react):
    points = kappa.shape[0]
    total_points = points * lax.axis_size("sea")
    index = lax.axis_index("sea") * points + jnp.arange(points, dtype=jnp.int32)
    left_k = jnp.concatenate([jnp.zeros((1,), kappa.dtype), kappa[:-1]])
    right_k = jnp.where(index == total_points - 1, 0.0, kappa)
    diag = left_k + right_k + react
    return left_k[:, None, None], right_k[:, None, None], diag[:, None, None]


def banded_smooth(motion, coefficients, halo):
    points = motion.shape[0]
    width = 2 * halo + 1
    rows = jnp.arange(points, dtype=jnp.int32)
    lanes = jnp.arange(width, dtype=jnp.int32)
    probe = (rows[:, None] % width == lanes[None, :]).astype(jnp.float32)[:, None, :]
    response = smooth(probe, *coefficients, 0)[:, 0, :]
    padded = jnp.pad(motion, ((halo, halo), (0, 0), (0, 0)))
    picks = (rows[None, :, None] + lanes[:, None, None] - halo) % width == lanes[None, None, :]
    bands = lax.optimization_barrier(jnp.sum(jnp.where(picks, response[None], 0.0), axis=2))
    total = None
    for offset in range(-halo, halo + 1):
        band = bands[offset + halo][:, None, None]
        term = band * padded[halo + offset : halo + offset + points].astype(jnp.float32)
        total = term if total is None else total + term
    return total


def smooth_with_edges(motion, halo_rows, coefficients, local_coefficients_, halo, banded=False):
    points = motion.shape[0]
    span = 3 * halo + 1
    keep = halo + 1
    if banded:
        interior = banded_smooth(motion, local_coefficients_, halo).astype(jnp.bfloat16)
    else:
        interior = smooth(motion.astype(jnp.float32), *local_coefficients_, 0).astype(jnp.bfloat16)
    before, after = halo_rows
    left_src = jnp.concatenate([before, motion[: span - halo]]).astype(jnp.float32)
    right_src = jnp.concatenate([motion[points - span + halo :], after]).astype(jnp.float32)
    left_k, right_k, diag = coefficients
    extent = left_k.shape[0]
    left = smooth(left_src, left_k[:span], right_k[:span], diag[:span], halo)
    right = smooth(
        right_src, left_k[extent - span :], right_k[extent - span :], diag[extent - span :], halo
    )
    interior = lax.dynamic_update_slice_in_dim(interior, left.astype(jnp.bfloat16), 0, 0)
    return lax.dynamic_update_slice_in_dim(
        interior, right.astype(jnp.bfloat16), points - keep, 0
    )


def dft_tables(steps_all):
    freq_ids = jnp.arange(steps_all, dtype=jnp.int32)
    phase_ids = freq_ids[:, None] * freq_ids[None, :] % steps_all
    angles = phase_ids.astype(jnp.float32) * (2.0 * math.pi / steps_all)
    scale = 1.0 / math.sqrt(steps_all)
    table = jnp.stack([jnp.cos(angles) * scale, -jnp.sin(angles) * scale], axis=1)
    table_high = lax.optimization_barrier(table.astype(jnp.bfloat16))
    table_low = (table - table_high.astype(jnp.float32)).astype(jnp.bfloat16)
    return table_high, table_low


def forward_chunk(prior_part, green, table_high, table_low):
    ways = lax.axis_size("tm")
    piece = lax.all_to_all(prior_part, "tm", split_axis=0, concat_axis=1, tiled=True)
    steps_all = piece.shape[1]
    high = table_high.reshape(ways, steps_all // ways, 2, steps_all)
    low = table_low.reshape(ways, steps_all // ways, 2, steps_all)
    spectrum = jnp.einsum("jfkt,qtc->jfkqc", high, piece, preferred_element_type=jnp.float32)
    spectrum = spectrum + jnp.einsum(
        "jfkt,qtc->jfkqc", low, piece, preferred_element_type=jnp.float32
    )
    spectrum = spectrum.astype(jnp.bfloat16)
    spectra = lax.all_to_all(spectrum, "tm", split_axis=0, concat_axis=0)
    real_s = spectra[:, :, 0]
    imag_s = spectra[:, :, 1]
    mixed = jnp.stack(
        [jnp.stack([real_s, imag_s], axis=2), jnp.stack([-imag_s, real_s], axis=2)], axis=0
    )
    blocks = green.reshape(green.shape[:3] + (ways, green.shape[3] // ways))
    partial = jnp.einsum("fksjq,kjfrqc->fsrc", blocks, mixed, preferred_element_type=jnp.float32)
    summed = lax.psum_scatter(partial.astype(jnp.bfloat16), "sea", scatter_dimension=1, tiled=True)
    return jnp.transpose(summed, (1, 0, 2, 3)).astype(jnp.float32)


def gathered_tables(blocks, steps_all):
    ways = lax.axis_size("tm")
    where_tm = lax.axis_index("tm").astype(jnp.int32)
    local = steps_all // ways
    freq_ids = where_tm * local + jnp.arange(local, dtype=jnp.int32)
    step_ids = (jnp.stack(blocks)[:, None] * local + jnp.arange(local, dtype=jnp.int32)).reshape(-1)
    phase_ids = freq_ids[:, None] * step_ids[None, :] % steps_all
    angles = phase_ids.astype(jnp.float32) * (2.0 * math.pi / steps_all)
    scale = 1.0 / math.sqrt(steps_all)
    real_w = jnp.cos(angles) * scale
    imag_w = -jnp.sin(angles) * scale
    table = jnp.stack(
        [jnp.stack([real_w, imag_w], axis=1), jnp.stack([-imag_w, real_w], axis=1)], axis=1
    )
    table_high = lax.optimization_barrier(table.astype(jnp.bfloat16))
    table_low = (table - table_high.astype(jnp.float32)).astype(jnp.bfloat16)
    return table_high, table_low


def gathered_spectrum(prior_part, after=None):
    where_tm = lax.axis_index("tm").astype(jnp.int32)
    chip_pairs = [(0, 1), (1, 0), (2, 3), (3, 2)]
    across = lax.ppermute(prior_part, "tm", [(0, 2), (2, 0), (1, 3), (3, 1)])
    partner = lax.ppermute(prior_part, "tm", chip_pairs)
    if after is not None:
        across, _ = lax.optimization_barrier((across, after))
    partner_across = lax.ppermute(across, "tm", chip_pairs)
    stacked = jnp.concatenate([prior_part, across, partner, partner_across], axis=1)
    blocks = [where_tm, where_tm ^ 2, where_tm ^ 1, where_tm ^ 3]
    steps_all = prior_part.shape[1] * len(blocks)
    table_high, _ = gathered_tables(blocks, steps_all)
    mixed = jnp.einsum("fkrt,ptc->fkrpc", table_high, stacked, preferred_element_type=jnp.float32)
    return mixed.astype(jnp.bfloat16)


def green_product(mixed, green):
    partial = jnp.einsum("fksp,fkrpc->fsrc", green, mixed, preferred_element_type=jnp.float32)
    summed = lax.psum_scatter(partial.astype(jnp.bfloat16), "sea", scatter_dimension=1, tiled=True)
    return jnp.transpose(summed, (1, 0, 2, 3)).astype(jnp.float32)


def on_device(motion, kappa, react, green):
    halo = SWEEPS - 1
    cols = motion.shape[2]
    width = cols // CHUNKS
    halo_rows, kappa_ext, react_ext = exchange_halo(motion, kappa, react, halo)
    coefficients = extended_coefficients(kappa_ext, react_ext, motion.shape[0], halo)
    inner = local_coefficients(kappa, react)
    priors = []
    for c in range(CHUNKS):
        part = slice(c * width, (c + 1) * width)
        source = motion[:, :, part]
        if priors:
            source, _ = lax.optimization_barrier((source, priors[-1]))
        rows = (halo_rows[0][:, :, part], halo_rows[1][:, :, part])
        priors.append(smooth_with_edges(source, rows, coefficients, inner, halo, c == 0))
    sensors = []
    if lax.axis_size("tm") == 4:
        spectra = []
        for c in range(CHUNKS):
            if c + 1 < CHUNKS:
                hold = (priors[c + 1],) + tuple(spectra[-1:])
            else:
                hold = tuple(spectra[-1:])
            mixed = gathered_spectrum(priors[c], hold if hold else None)
            spectra.append(mixed)
            sensors.append(green_product(mixed, green))
    else:
        table_high, table_low = dft_tables(motion.shape[1] * lax.axis_size("tm"))
        for prior_part in priors:
            sensors.append(forward_chunk(prior_part, green, table_high, table_low))
    return (jnp.concatenate(priors, axis=2), jnp.concatenate(sensors, axis=3))


def solution(mesh):
    in_specs = (P("sea", "tm", None), P("sea"), P("sea"), P("tm", None, None, "sea"))
    out_specs = (P("sea", "tm", None), P("sea", "tm", None, None))
    return jax.shard_map(
        on_device, mesh=mesh, in_specs=in_specs, out_specs=out_specs, check_vma=False
    )
```

```python
import math

import jax
import jax.numpy as jnp
from jax import lax
from jax.sharding import PartitionSpec as P

SWEEPS = 6
CHUNKS = 2


def from_left(block, axis):
    count = lax.axis_size(axis)
    return lax.ppermute(block, axis, [(i, i + 1) for i in range(count - 1)])


def from_right(block, axis):
    count = lax.axis_size(axis)
    return lax.ppermute(block, axis, [(i + 1, i) for i in range(count - 1)])


def omega_table(count):
    return [
        1.0 / (1.05 + 0.95 * math.cos((2 * k + 1) * math.pi / (2 * count))) for k in range(count)
    ]


def exchange_halo(motion, kappa, react, halo):
    points = motion.shape[0]
    shape = (halo,) + motion.shape[1:]
    size = math.prod(shape)
    tail = jnp.concatenate(
        [motion[points - halo :].astype(jnp.float32).reshape(-1), kappa[points - halo - 1 :], react[points - halo :]]
    )
    head = jnp.concatenate(
        [motion[:halo].astype(jnp.float32).reshape(-1), kappa[:halo], react[:halo]]
    )
    before = from_left(tail, "sea")
    after = from_right(head, "sea")
    halo_rows = (
        before[:size].reshape(shape).astype(motion.dtype),
        after[:size].reshape(shape).astype(motion.dtype),
    )
    kappa_ext = jnp.concatenate([before[size : size + halo + 1], kappa, after[size : size + halo]])
    react_ext = jnp.concatenate([before[size + halo + 1 :], react, after[size + halo :]])
    return halo_rows, kappa_ext, react_ext


def extended_coefficients(kappa_ext, react_ext, points, halo):
    groups = lax.axis_size("sea")
    total_points = points * groups
    where_sea = lax.axis_index("sea")
    index = where_sea * points - halo + jnp.arange(points + 2 * halo, dtype=jnp.int32)
    valid = (index >= 0) & (index < total_points)
    left_k = jnp.where(valid & (index >= 1), kappa_ext[:-1], 0.0)
    right_k = jnp.where(valid & (index < total_points - 1), kappa_ext[1:], 0.0)
    react_v = jnp.where(valid, react_ext, 1.0)
    diag = left_k + right_k + react_v
    return left_k[:, None, None], right_k[:, None, None], diag[:, None, None]


def smooth(source, left_k, right_k, diag, halo):
    weights = omega_table(SWEEPS)
    state = weights[0] * source / diag
    for k in range(1, SWEEPS):
        padded = jnp.pad(state, ((1, 1), (0, 0), (0, 0)))
        applied = diag * state - left_k * padded[:-2] - right_k * padded[2:]
        state = state + weights[k] * (source - applied) / diag
    return state[halo : state.shape[0] - halo]


def local_coefficients(kappa, react):
    points = kappa.shape[0]
    total_points = points * lax.axis_size("sea")
    index = lax.axis_index("sea") * points + jnp.arange(points, dtype=jnp.int32)
    left_k = jnp.concatenate([jnp.zeros((1,), kappa.dtype), kappa[:-1]])
    right_k = jnp.where(index == total_points - 1, 0.0, kappa)
    diag = left_k + right_k + react
    return left_k[:, None, None], right_k[:, None, None], diag[:, None, None]


def banded_smooth(motion, coefficients, halo):
    points = motion.shape[0]
    width = 2 * halo + 1
    rows = jnp.arange(points, dtype=jnp.int32)
    lanes = jnp.arange(width, dtype=jnp.int32)
    probe = (rows[:, None] % width == lanes[None, :]).astype(jnp.float32)[:, None, :]
    response = smooth(probe, *coefficients, 0)[:, 0, :]
    picks = (rows[None, :, None] + lanes[:, None, None] - halo) % width == lanes[None, None, :]
    bands = lax.optimization_barrier(jnp.sum(jnp.where(picks, response[None], 0.0), axis=2))
    inner = points - 2 * halo
    total = None
    for offset in range(-halo, halo + 1):
        band = bands[offset + halo, halo : halo + inner][:, None, None]
        term = band * motion[halo + offset : halo + offset + inner].astype(jnp.float32)
        total = term if total is None else total + term
    return jnp.pad(total, ((halo, halo), (0, 0), (0, 0)))


def smooth_with_edges(motion, halo_rows, coefficients, local_coefficients_, halo, banded=False):
    points = motion.shape[0]
    span = 3 * halo + 1
    keep = halo + 1
    if banded:
        interior = banded_smooth(motion, local_coefficients_, halo).astype(jnp.bfloat16)
    else:
        interior = smooth(motion.astype(jnp.float32), *local_coefficients_, 0).astype(jnp.bfloat16)
    before, after = halo_rows
    left_src = jnp.concatenate([before, motion[: span - halo]]).astype(jnp.float32)
    right_src = jnp.concatenate([motion[points - span + halo :], after]).astype(jnp.float32)
    left_k, right_k, diag = coefficients
    extent = left_k.shape[0]
    left = smooth(left_src, left_k[:span], right_k[:span], diag[:span], halo)
    right = smooth(
        right_src, left_k[extent - span :], right_k[extent - span :], diag[extent - span :], halo
    )
    interior = lax.dynamic_update_slice_in_dim(interior, left.astype(jnp.bfloat16), 0, 0)
    return lax.dynamic_update_slice_in_dim(
        interior, right.astype(jnp.bfloat16), points - keep, 0
    )


def dft_tables(steps_all):
    freq_ids = jnp.arange(steps_all, dtype=jnp.int32)
    phase_ids = freq_ids[:, None] * freq_ids[None, :] % steps_all
    angles = phase_ids.astype(jnp.float32) * (2.0 * math.pi / steps_all)
    scale = 1.0 / math.sqrt(steps_all)
    table = jnp.stack([jnp.cos(angles) * scale, -jnp.sin(angles) * scale], axis=1)
    table_high = lax.optimization_barrier(table.astype(jnp.bfloat16))
    table_low = (table - table_high.astype(jnp.float32)).astype(jnp.bfloat16)
    return table_high, table_low


def forward_chunk(prior_part, green, table_high, table_low):
    ways = lax.axis_size("tm")
    piece = lax.all_to_all(prior_part, "tm", split_axis=0, concat_axis=1, tiled=True)
    steps_all = piece.shape[1]
    high = table_high.reshape(ways, steps_all // ways, 2, steps_all)
    low = table_low.reshape(ways, steps_all // ways, 2, steps_all)
    spectrum = jnp.einsum("jfkt,qtc->jfkqc", high, piece, preferred_element_type=jnp.float32)
    spectrum = spectrum + jnp.einsum(
        "jfkt,qtc->jfkqc", low, piece, preferred_element_type=jnp.float32
    )
    spectrum = spectrum.astype(jnp.bfloat16)
    spectra = lax.all_to_all(spectrum, "tm", split_axis=0, concat_axis=0)
    real_s = spectra[:, :, 0]
    imag_s = spectra[:, :, 1]
    mixed = jnp.stack(
        [jnp.stack([real_s, imag_s], axis=2), jnp.stack([-imag_s, real_s], axis=2)], axis=0
    )
    blocks = green.reshape(green.shape[:3] + (ways, green.shape[3] // ways))
    partial = jnp.einsum("fksjq,kjfrqc->fsrc", blocks, mixed, preferred_element_type=jnp.float32)
    summed = lax.psum_scatter(partial.astype(jnp.bfloat16), "sea", scatter_dimension=1, tiled=True)
    return jnp.transpose(summed, (1, 0, 2, 3)).astype(jnp.float32)


def gathered_tables(blocks, steps_all):
    ways = lax.axis_size("tm")
    where_tm = lax.axis_index("tm").astype(jnp.int32)
    local = steps_all // ways
    freq_ids = where_tm * local + jnp.arange(local, dtype=jnp.int32)
    step_ids = (jnp.stack(blocks)[:, None] * local + jnp.arange(local, dtype=jnp.int32)).reshape(-1)
    phase_ids = freq_ids[:, None] * step_ids[None, :] % steps_all
    angles = phase_ids.astype(jnp.float32) * (2.0 * math.pi / steps_all)
    scale = 1.0 / math.sqrt(steps_all)
    real_w = jnp.cos(angles) * scale
    imag_w = -jnp.sin(angles) * scale
    table = jnp.stack(
        [jnp.stack([real_w, imag_w], axis=1), jnp.stack([-imag_w, real_w], axis=1)], axis=1
    )
    table_high = lax.optimization_barrier(table.astype(jnp.bfloat16))
    table_low = (table - table_high.astype(jnp.float32)).astype(jnp.bfloat16)
    return table_high, table_low


def gathered_spectrum(prior_part, after=None):
    where_tm = lax.axis_index("tm").astype(jnp.int32)
    chip_pairs = [(0, 1), (1, 0), (2, 3), (3, 2)]
    across = lax.ppermute(prior_part, "tm", [(0, 2), (2, 0), (1, 3), (3, 1)])
    partner = lax.ppermute(prior_part, "tm", chip_pairs)
    if after is not None:
        across, _ = lax.optimization_barrier((across, after))
    partner_across = lax.ppermute(across, "tm", chip_pairs)
    stacked = jnp.concatenate([prior_part, across, partner, partner_across], axis=1)
    blocks = [where_tm, where_tm ^ 2, where_tm ^ 1, where_tm ^ 3]
    steps_all = prior_part.shape[1] * len(blocks)
    table_high, _ = gathered_tables(blocks, steps_all)
    mixed = jnp.einsum("fkrt,ptc->fkrpc", table_high, stacked, preferred_element_type=jnp.float32)
    return mixed.astype(jnp.bfloat16)


def green_product(mixed, green):
    partial = jnp.einsum("fksp,fkrpc->fsrc", green, mixed, preferred_element_type=jnp.float32)
    summed = lax.psum_scatter(partial.astype(jnp.bfloat16), "sea", scatter_dimension=1, tiled=True)
    return jnp.transpose(summed, (1, 0, 2, 3)).astype(jnp.float32)


def on_device(motion, kappa, react, green):
    halo = SWEEPS - 1
    cols = motion.shape[2]
    width = cols // CHUNKS
    halo_rows, kappa_ext, react_ext = exchange_halo(motion, kappa, react, halo)
    coefficients = extended_coefficients(kappa_ext, react_ext, motion.shape[0], halo)
    inner = local_coefficients(kappa, react)
    priors = []
    for c in range(CHUNKS):
        part = slice(c * width, (c + 1) * width)
        source = motion[:, :, part]
        if priors:
            source, _ = lax.optimization_barrier((source, priors[-1]))
        rows = (halo_rows[0][:, :, part], halo_rows[1][:, :, part])
        priors.append(smooth_with_edges(source, rows, coefficients, inner, halo, c == 0))
    sensors = []
    if lax.axis_size("tm") == 4:
        spectra = []
        for c in range(CHUNKS):
            if c + 1 < CHUNKS:
                hold = (priors[c + 1],) + tuple(spectra[-1:])
            else:
                hold = tuple(spectra[-1:])
            mixed = gathered_spectrum(priors[c], hold if hold else None)
            spectra.append(mixed)
            sensors.append(green_product(mixed, green))
    else:
        table_high, table_low = dft_tables(motion.shape[1] * lax.axis_size("tm"))
        for prior_part in priors:
            sensors.append(forward_chunk(prior_part, green, table_high, table_low))
    return (jnp.concatenate(priors, axis=2), jnp.concatenate(sensors, axis=3))


def solution(mesh):
    in_specs = (P("sea", "tm", None), P("sea"), P("sea"), P("tm", None, None, "sea"))
    out_specs = (P("sea", "tm", None), P("sea", "tm", None, None))
    return jax.shard_map(
        on_device, mesh=mesh, in_specs=in_specs, out_specs=out_specs, check_vma=False
    )
```

```python
import math

import jax
import jax.numpy as jnp
from jax import lax
from jax.sharding import PartitionSpec as P

SWEEPS = 6
CHUNKS = 2


def from_left(block, axis):
    count = lax.axis_size(axis)
    return lax.ppermute(block, axis, [(i, i + 1) for i in range(count - 1)])


def from_right(block, axis):
    count = lax.axis_size(axis)
    return lax.ppermute(block, axis, [(i + 1, i) for i in range(count - 1)])


def omega_table(count):
    return [
        1.0 / (1.05 + 0.95 * math.cos((2 * k + 1) * math.pi / (2 * count))) for k in range(count)
    ]


def exchange_halo(motion, kappa, react, halo):
    points = motion.shape[0]
    shape = (halo,) + motion.shape[1:]
    size = math.prod(shape)
    tail = jnp.concatenate(
        [motion[points - halo :].astype(jnp.float32).reshape(-1), kappa[points - halo - 1 :], react[points - halo :]]
    )
    head = jnp.concatenate(
        [motion[:halo].astype(jnp.float32).reshape(-1), kappa[:halo], react[:halo]]
    )
    before = from_left(tail, "sea")
    after = from_right(head, "sea")
    halo_rows = (
        before[:size].reshape(shape).astype(motion.dtype),
        after[:size].reshape(shape).astype(motion.dtype),
    )
    kappa_ext = jnp.concatenate([before[size : size + halo + 1], kappa, after[size : size + halo]])
    react_ext = jnp.concatenate([before[size + halo + 1 :], react, after[size + halo :]])
    return halo_rows, kappa_ext, react_ext


def extended_coefficients(kappa_ext, react_ext, points, halo):
    groups = lax.axis_size("sea")
    total_points = points * groups
    where_sea = lax.axis_index("sea")
    index = where_sea * points - halo + jnp.arange(points + 2 * halo, dtype=jnp.int32)
    valid = (index >= 0) & (index < total_points)
    left_k = jnp.where(valid & (index >= 1), kappa_ext[:-1], 0.0)
    right_k = jnp.where(valid & (index < total_points - 1), kappa_ext[1:], 0.0)
    react_v = jnp.where(valid, react_ext, 1.0)
    diag = left_k + right_k + react_v
    return left_k[:, None, None], right_k[:, None, None], diag[:, None, None]


def smooth(source, left_k, right_k, diag, halo):
    weights = omega_table(SWEEPS)
    state = weights[0] * source / diag
    for k in range(1, SWEEPS):
        padded = jnp.pad(state, ((1, 1), (0, 0), (0, 0)))
        applied = diag * state - left_k * padded[:-2] - right_k * padded[2:]
        state = state + weights[k] * (source - applied) / diag
    return state[halo : state.shape[0] - halo]


def local_coefficients(kappa, react):
    points = kappa.shape[0]
    total_points = points * lax.axis_size("sea")
    index = lax.axis_index("sea") * points + jnp.arange(points, dtype=jnp.int32)
    left_k = jnp.concatenate([jnp.zeros((1,), kappa.dtype), kappa[:-1]])
    right_k = jnp.where(index == total_points - 1, 0.0, kappa)
    diag = left_k + right_k + react
    return left_k[:, None, None], right_k[:, None, None], diag[:, None, None]


def banded_smooth(motion, coefficients, halo):
    points = motion.shape[0]
    width = 2 * halo + 1
    rows = jnp.arange(points, dtype=jnp.int32)
    lanes = jnp.arange(width, dtype=jnp.int32)
    probe = (rows[:, None] % width == lanes[None, :]).astype(jnp.float32)[:, None, :]
    response = smooth(probe, *coefficients, 0)[:, 0, :]
    picks = (rows[None, :, None] + lanes[:, None, None] - halo) % width == lanes[None, None, :]
    bands = lax.optimization_barrier(jnp.sum(jnp.where(picks, response[None], 0.0), axis=2))
    inner = points - 2 * halo
    total = None
    for offset in range(-halo, halo + 1):
        band = bands[offset + halo, halo : halo + inner][:, None, None]
        term = band * motion[halo + offset : halo + offset + inner].astype(jnp.float32)
        total = term if total is None else total + term
    return total


def smooth_with_edges(motion, halo_rows, coefficients, local_coefficients_, halo, banded=False):
    points = motion.shape[0]
    span = 3 * halo + 1
    keep = halo + 1
    if banded:
        inner = banded_smooth(motion, local_coefficients_, halo)[1 : points - 2 * halo - 1]
    else:
        interior = smooth(motion.astype(jnp.float32), *local_coefficients_, 0).astype(jnp.bfloat16)
    before, after = halo_rows
    left_src = jnp.concatenate([before, motion[: span - halo]]).astype(jnp.float32)
    right_src = jnp.concatenate([motion[points - span + halo :], after]).astype(jnp.float32)
    left_k, right_k, diag = coefficients
    extent = left_k.shape[0]
    left = smooth(left_src, left_k[:span], right_k[:span], diag[:span], halo)
    right = smooth(
        right_src, left_k[extent - span :], right_k[extent - span :], diag[extent - span :], halo
    )
    if banded:
        return jnp.concatenate([left, inner, right]).astype(jnp.bfloat16)
    interior = lax.dynamic_update_slice_in_dim(interior, left.astype(jnp.bfloat16), 0, 0)
    return lax.dynamic_update_slice_in_dim(
        interior, right.astype(jnp.bfloat16), points - keep, 0
    )


def dft_tables(steps_all):
    freq_ids = jnp.arange(steps_all, dtype=jnp.int32)
    phase_ids = freq_ids[:, None] * freq_ids[None, :] % steps_all
    angles = phase_ids.astype(jnp.float32) * (2.0 * math.pi / steps_all)
    scale = 1.0 / math.sqrt(steps_all)
    table = jnp.stack([jnp.cos(angles) * scale, -jnp.sin(angles) * scale], axis=1)
    table_high = lax.optimization_barrier(table.astype(jnp.bfloat16))
    table_low = (table - table_high.astype(jnp.float32)).astype(jnp.bfloat16)
    return table_high, table_low


def forward_chunk(prior_part, green, table_high, table_low):
    ways = lax.axis_size("tm")
    piece = lax.all_to_all(prior_part, "tm", split_axis=0, concat_axis=1, tiled=True)
    steps_all = piece.shape[1]
    high = table_high.reshape(ways, steps_all // ways, 2, steps_all)
    low = table_low.reshape(ways, steps_all // ways, 2, steps_all)
    spectrum = jnp.einsum("jfkt,qtc->jfkqc", high, piece, preferred_element_type=jnp.float32)
    spectrum = spectrum + jnp.einsum(
        "jfkt,qtc->jfkqc", low, piece, preferred_element_type=jnp.float32
    )
    spectrum = spectrum.astype(jnp.bfloat16)
    spectra = lax.all_to_all(spectrum, "tm", split_axis=0, concat_axis=0)
    real_s = spectra[:, :, 0]
    imag_s = spectra[:, :, 1]
    mixed = jnp.stack(
        [jnp.stack([real_s, imag_s], axis=2), jnp.stack([-imag_s, real_s], axis=2)], axis=0
    )
    blocks = green.reshape(green.shape[:3] + (ways, green.shape[3] // ways))
    partial = jnp.einsum("fksjq,kjfrqc->fsrc", blocks, mixed, preferred_element_type=jnp.float32)
    summed = lax.psum_scatter(partial.astype(jnp.bfloat16), "sea", scatter_dimension=1, tiled=True)
    return jnp.transpose(summed, (1, 0, 2, 3)).astype(jnp.float32)


def gathered_tables(blocks, steps_all):
    ways = lax.axis_size("tm")
    where_tm = lax.axis_index("tm").astype(jnp.int32)
    local = steps_all // ways
    freq_ids = where_tm * local + jnp.arange(local, dtype=jnp.int32)
    step_ids = (jnp.stack(blocks)[:, None] * local + jnp.arange(local, dtype=jnp.int32)).reshape(-1)
    phase_ids = freq_ids[:, None] * step_ids[None, :] % steps_all
    angles = phase_ids.astype(jnp.float32) * (2.0 * math.pi / steps_all)
    scale = 1.0 / math.sqrt(steps_all)
    real_w = jnp.cos(angles) * scale
    imag_w = -jnp.sin(angles) * scale
    table = jnp.stack(
        [jnp.stack([real_w, imag_w], axis=1), jnp.stack([-imag_w, real_w], axis=1)], axis=1
    )
    table_high = lax.optimization_barrier(table.astype(jnp.bfloat16))
    table_low = (table - table_high.astype(jnp.float32)).astype(jnp.bfloat16)
    return table_high, table_low


def gathered_spectrum(prior_part, after=None):
    where_tm = lax.axis_index("tm").astype(jnp.int32)
    chip_pairs = [(0, 1), (1, 0), (2, 3), (3, 2)]
    across = lax.ppermute(prior_part, "tm", [(0, 2), (2, 0), (1, 3), (3, 1)])
    partner = lax.ppermute(prior_part, "tm", chip_pairs)
    if after is not None:
        across, _ = lax.optimization_barrier((across, after))
    partner_across = lax.ppermute(across, "tm", chip_pairs)
    stacked = jnp.concatenate([prior_part, across, partner, partner_across], axis=1)
    blocks = [where_tm, where_tm ^ 2, where_tm ^ 1, where_tm ^ 3]
    steps_all = prior_part.shape[1] * len(blocks)
    table_high, _ = gathered_tables(blocks, steps_all)
    mixed = jnp.einsum("fkrt,ptc->fkrpc", table_high, stacked, preferred_element_type=jnp.float32)
    return mixed.astype(jnp.bfloat16)


def green_product(mixed, green):
    partial = jnp.einsum("fksp,fkrpc->fsrc", green, mixed, preferred_element_type=jnp.float32)
    summed = lax.psum_scatter(partial.astype(jnp.bfloat16), "sea", scatter_dimension=1, tiled=True)
    return jnp.transpose(summed, (1, 0, 2, 3)).astype(jnp.float32)


def on_device(motion, kappa, react, green):
    halo = SWEEPS - 1
    cols = motion.shape[2]
    width = cols // CHUNKS
    halo_rows, kappa_ext, react_ext = exchange_halo(motion, kappa, react, halo)
    coefficients = extended_coefficients(kappa_ext, react_ext, motion.shape[0], halo)
    inner = local_coefficients(kappa, react)
    priors = []
    for c in range(CHUNKS):
        part = slice(c * width, (c + 1) * width)
        source = motion[:, :, part]
        if priors:
            source, _ = lax.optimization_barrier((source, priors[-1]))
        rows = (halo_rows[0][:, :, part], halo_rows[1][:, :, part])
        priors.append(smooth_with_edges(source, rows, coefficients, inner, halo, c == 0))
    sensors = []
    if lax.axis_size("tm") == 4:
        spectra = []
        for c in range(CHUNKS):
            if c + 1 < CHUNKS:
                hold = (priors[c + 1],) + tuple(spectra[-1:])
            else:
                hold = tuple(spectra[-1:])
            mixed = gathered_spectrum(priors[c], hold if hold else None)
            spectra.append(mixed)
            sensors.append(green_product(mixed, green))
    else:
        table_high, table_low = dft_tables(motion.shape[1] * lax.axis_size("tm"))
        for prior_part in priors:
            sensors.append(forward_chunk(prior_part, green, table_high, table_low))
    return (jnp.concatenate(priors, axis=2), jnp.concatenate(sensors, axis=3))


def solution(mesh):
    in_specs = (P("sea", "tm", None), P("sea"), P("sea"), P("tm", None, None, "sea"))
    out_specs = (P("sea", "tm", None), P("sea", "tm", None, None))
    return jax.shard_map(
        on_device, mesh=mesh, in_specs=in_specs, out_specs=out_specs, check_vma=False
    )
```

```python
import math

import jax
import jax.numpy as jnp
from jax import lax
from jax.sharding import PartitionSpec as P

SWEEPS = 6
CHUNKS = 2


def from_left(block, axis):
    count = lax.axis_size(axis)
    return lax.ppermute(block, axis, [(i, i + 1) for i in range(count - 1)])


def from_right(block, axis):
    count = lax.axis_size(axis)
    return lax.ppermute(block, axis, [(i + 1, i) for i in range(count - 1)])


def omega_table(count):
    return [
        1.0 / (1.05 + 0.95 * math.cos((2 * k + 1) * math.pi / (2 * count))) for k in range(count)
    ]


def exchange_halo(motion, kappa, react, halo):
    points = motion.shape[0]
    shape = (halo,) + motion.shape[1:]
    size = math.prod(shape)
    tail = jnp.concatenate(
        [motion[points - halo :].astype(jnp.float32).reshape(-1), kappa[points - halo - 1 :], react[points - halo :]]
    )
    head = jnp.concatenate(
        [motion[:halo].astype(jnp.float32).reshape(-1), kappa[:halo], react[:halo]]
    )
    before = from_left(tail, "sea")
    after = from_right(head, "sea")
    halo_rows = (
        before[:size].reshape(shape).astype(motion.dtype),
        after[:size].reshape(shape).astype(motion.dtype),
    )
    kappa_ext = jnp.concatenate([before[size : size + halo + 1], kappa, after[size : size + halo]])
    react_ext = jnp.concatenate([before[size + halo + 1 :], react, after[size + halo :]])
    return halo_rows, kappa_ext, react_ext


def extended_coefficients(kappa_ext, react_ext, points, halo):
    groups = lax.axis_size("sea")
    total_points = points * groups
    where_sea = lax.axis_index("sea")
    index = where_sea * points - halo + jnp.arange(points + 2 * halo, dtype=jnp.int32)
    valid = (index >= 0) & (index < total_points)
    left_k = jnp.where(valid & (index >= 1), kappa_ext[:-1], 0.0)
    right_k = jnp.where(valid & (index < total_points - 1), kappa_ext[1:], 0.0)
    react_v = jnp.where(valid, react_ext, 1.0)
    diag = left_k + right_k + react_v
    return left_k[:, None, None], right_k[:, None, None], diag[:, None, None]


def smooth(source, left_k, right_k, diag, halo):
    weights = omega_table(SWEEPS)
    state = weights[0] * source / diag
    for k in range(1, SWEEPS):
        padded = jnp.pad(state, ((1, 1), (0, 0), (0, 0)))
        applied = diag * state - left_k * padded[:-2] - right_k * padded[2:]
        state = state + weights[k] * (source - applied) / diag
    return state[halo : state.shape[0] - halo]


def local_coefficients(kappa, react):
    points = kappa.shape[0]
    total_points = points * lax.axis_size("sea")
    index = lax.axis_index("sea") * points + jnp.arange(points, dtype=jnp.int32)
    left_k = jnp.concatenate([jnp.zeros((1,), kappa.dtype), kappa[:-1]])
    right_k = jnp.where(index == total_points - 1, 0.0, kappa)
    diag = left_k + right_k + react
    return left_k[:, None, None], right_k[:, None, None], diag[:, None, None]


def banded_smooth(motion, coefficients, halo):
    points = motion.shape[0]
    width = 2 * halo + 1
    rows = jnp.arange(points, dtype=jnp.int32)
    lanes = jnp.arange(width, dtype=jnp.int32)
    probe = (rows[:, None] % width == lanes[None, :]).astype(jnp.float32)[:, None, :]
    response = smooth(probe, *coefficients, 0)[:, 0, :]
    picks = (rows[None, :, None] + lanes[:, None, None] - halo) % width == lanes[None, None, :]
    bands = lax.optimization_barrier(jnp.sum(jnp.where(picks, response[None], 0.0), axis=2))
    inner = points - 2 * halo
    total = None
    for offset in range(-halo, halo + 1):
        band = bands[offset + halo, halo : halo + inner][:, None, None]
        term = band * motion[halo + offset : halo + offset + inner].astype(jnp.float32)
        total = term if total is None else total + term
    return jnp.pad(total, ((halo, halo), (0, 0), (0, 0)))


def edge_rows(motion, halo_rows, coefficients, halo):
    points = motion.shape[0]
    span = 3 * halo + 1
    before, after = halo_rows
    left_src = jnp.concatenate([before, motion[: span - halo]]).astype(jnp.float32)
    right_src = jnp.concatenate([motion[points - span + halo :], after]).astype(jnp.float32)
    left_k, right_k, diag = coefficients
    extent = left_k.shape[0]
    left = smooth(left_src, left_k[:span], right_k[:span], diag[:span], halo)
    right = smooth(
        right_src, left_k[extent - span :], right_k[extent - span :], diag[extent - span :], halo
    )
    return left.astype(jnp.bfloat16), right.astype(jnp.bfloat16)


def smooth_with_edges(motion, edges, local_coefficients_, halo, banded=False):
    points = motion.shape[0]
    keep = halo + 1
    if banded:
        interior = banded_smooth(motion, local_coefficients_, halo).astype(jnp.bfloat16)
    else:
        interior = smooth(motion.astype(jnp.float32), *local_coefficients_, 0).astype(jnp.bfloat16)
    left, right = edges
    interior = lax.dynamic_update_slice_in_dim(interior, left, 0, 0)
    return lax.dynamic_update_slice_in_dim(interior, right, points - keep, 0)


def dft_tables(steps_all):
    freq_ids = jnp.arange(steps_all, dtype=jnp.int32)
    phase_ids = freq_ids[:, None] * freq_ids[None, :] % steps_all
    angles = phase_ids.astype(jnp.float32) * (2.0 * math.pi / steps_all)
    scale = 1.0 / math.sqrt(steps_all)
    table = jnp.stack([jnp.cos(angles) * scale, -jnp.sin(angles) * scale], axis=1)
    table_high = lax.optimization_barrier(table.astype(jnp.bfloat16))
    table_low = (table - table_high.astype(jnp.float32)).astype(jnp.bfloat16)
    return table_high, table_low


def forward_chunk(prior_part, green, table_high, table_low):
    ways = lax.axis_size("tm")
    piece = lax.all_to_all(prior_part, "tm", split_axis=0, concat_axis=1, tiled=True)
    steps_all = piece.shape[1]
    high = table_high.reshape(ways, steps_all // ways, 2, steps_all)
    low = table_low.reshape(ways, steps_all // ways, 2, steps_all)
    spectrum = jnp.einsum("jfkt,qtc->jfkqc", high, piece, preferred_element_type=jnp.float32)
    spectrum = spectrum + jnp.einsum(
        "jfkt,qtc->jfkqc", low, piece, preferred_element_type=jnp.float32
    )
    spectrum = spectrum.astype(jnp.bfloat16)
    spectra = lax.all_to_all(spectrum, "tm", split_axis=0, concat_axis=0)
    real_s = spectra[:, :, 0]
    imag_s = spectra[:, :, 1]
    mixed = jnp.stack(
        [jnp.stack([real_s, imag_s], axis=2), jnp.stack([-imag_s, real_s], axis=2)], axis=0
    )
    blocks = green.reshape(green.shape[:3] + (ways, green.shape[3] // ways))
    partial = jnp.einsum("fksjq,kjfrqc->fsrc", blocks, mixed, preferred_element_type=jnp.float32)
    summed = lax.psum_scatter(partial.astype(jnp.bfloat16), "sea", scatter_dimension=1, tiled=True)
    return jnp.transpose(summed, (1, 0, 2, 3)).astype(jnp.float32)


def gathered_tables(blocks, steps_all):
    ways = lax.axis_size("tm")
    where_tm = lax.axis_index("tm").astype(jnp.int32)
    local = steps_all // ways
    freq_ids = where_tm * local + jnp.arange(local, dtype=jnp.int32)
    step_ids = (jnp.stack(blocks)[:, None] * local + jnp.arange(local, dtype=jnp.int32)).reshape(-1)
    phase_ids = freq_ids[:, None] * step_ids[None, :] % steps_all
    angles = phase_ids.astype(jnp.float32) * (2.0 * math.pi / steps_all)
    scale = 1.0 / math.sqrt(steps_all)
    real_w = jnp.cos(angles) * scale
    imag_w = -jnp.sin(angles) * scale
    table = jnp.stack(
        [jnp.stack([real_w, imag_w], axis=1), jnp.stack([-imag_w, real_w], axis=1)], axis=1
    )
    table_high = lax.optimization_barrier(table.astype(jnp.bfloat16))
    table_low = (table - table_high.astype(jnp.float32)).astype(jnp.bfloat16)
    return table_high, table_low


def gathered_spectrum(prior_part, after=None):
    where_tm = lax.axis_index("tm").astype(jnp.int32)
    chip_pairs = [(0, 1), (1, 0), (2, 3), (3, 2)]
    across = lax.ppermute(prior_part, "tm", [(0, 2), (2, 0), (1, 3), (3, 1)])
    partner = lax.ppermute(prior_part, "tm", chip_pairs)
    if after is not None:
        across, _ = lax.optimization_barrier((across, after))
    partner_across = lax.ppermute(across, "tm", chip_pairs)
    stacked = jnp.concatenate([prior_part, across, partner, partner_across], axis=1)
    blocks = [where_tm, where_tm ^ 2, where_tm ^ 1, where_tm ^ 3]
    steps_all = prior_part.shape[1] * len(blocks)
    table_high, _ = gathered_tables(blocks, steps_all)
    mixed = jnp.einsum("fkrt,ptc->fkrpc", table_high, stacked, preferred_element_type=jnp.float32)
    return mixed.astype(jnp.bfloat16)


def green_product(mixed, green):
    partial = jnp.einsum("fksp,fkrpc->fsrc", green, mixed, preferred_element_type=jnp.float32)
    summed = lax.psum_scatter(partial.astype(jnp.bfloat16), "sea", scatter_dimension=1, tiled=True)
    return jnp.transpose(summed, (1, 0, 2, 3)).astype(jnp.float32)


def on_device(motion, kappa, react, green):
    halo = SWEEPS - 1
    cols = motion.shape[2]
    width = cols // CHUNKS
    halo_rows, kappa_ext, react_ext = exchange_halo(motion, kappa, react, halo)
    coefficients = extended_coefficients(kappa_ext, react_ext, motion.shape[0], halo)
    inner = local_coefficients(kappa, react)
    left_all, right_all = edge_rows(motion, halo_rows, coefficients, halo)
    priors = []
    for c in range(CHUNKS):
        part = slice(c * width, (c + 1) * width)
        source = motion[:, :, part]
        if priors:
            source, _ = lax.optimization_barrier((source, priors[-1]))
        edges = (left_all[:, :, part], right_all[:, :, part])
        priors.append(smooth_with_edges(source, edges, inner, halo, c == 0))
    sensors = []
    if lax.axis_size("tm") == 4:
        spectra = []
        for c in range(CHUNKS):
            if c + 1 < CHUNKS:
                hold = (priors[c + 1],) + tuple(spectra[-1:])
            else:
                hold = tuple(spectra[-1:])
            mixed = gathered_spectrum(priors[c], hold if hold else None)
            spectra.append(mixed)
            sensors.append(green_product(mixed, green))
    else:
        table_high, table_low = dft_tables(motion.shape[1] * lax.axis_size("tm"))
        for prior_part in priors:
            sensors.append(forward_chunk(prior_part, green, table_high, table_low))
    return (jnp.concatenate(priors, axis=2), jnp.concatenate(sensors, axis=3))


def solution(mesh):
    in_specs = (P("sea", "tm", None), P("sea"), P("sea"), P("tm", None, None, "sea"))
    out_specs = (P("sea", "tm", None), P("sea", "tm", None, None))
    return jax.shard_map(
        on_device, mesh=mesh, in_specs=in_specs, out_specs=out_specs, check_vma=False
    )
```

```python
import math

import jax
import jax.numpy as jnp
from jax import lax
from jax.sharding import PartitionSpec as P

SWEEPS = 6
CHUNKS = 2


def from_left(block, axis):
    count = lax.axis_size(axis)
    return lax.ppermute(block, axis, [(i, i + 1) for i in range(count - 1)])


def from_right(block, axis):
    count = lax.axis_size(axis)
    return lax.ppermute(block, axis, [(i + 1, i) for i in range(count - 1)])


def omega_table(count):
    return [
        1.0 / (1.05 + 0.95 * math.cos((2 * k + 1) * math.pi / (2 * count))) for k in range(count)
    ]


def exchange_halo(motion, kappa, react, halo):
    points = motion.shape[0]
    shape = (halo,) + motion.shape[1:]
    size = math.prod(shape)
    tail = jnp.concatenate(
        [motion[points - halo :].astype(jnp.float32).reshape(-1), kappa[points - halo - 1 :], react[points - halo :]]
    )
    head = jnp.concatenate(
        [motion[:halo].astype(jnp.float32).reshape(-1), kappa[:halo], react[:halo]]
    )
    before = from_left(tail, "sea")
    after = from_right(head, "sea")
    halo_rows = (
        before[:size].reshape(shape).astype(motion.dtype),
        after[:size].reshape(shape).astype(motion.dtype),
    )
    kappa_ext = jnp.concatenate([before[size : size + halo + 1], kappa, after[size : size + halo]])
    react_ext = jnp.concatenate([before[size + halo + 1 :], react, after[size + halo :]])
    return halo_rows, kappa_ext, react_ext


def extended_coefficients(kappa_ext, react_ext, points, halo):
    groups = lax.axis_size("sea")
    total_points = points * groups
    where_sea = lax.axis_index("sea")
    index = where_sea * points - halo + jnp.arange(points + 2 * halo, dtype=jnp.int32)
    valid = (index >= 0) & (index < total_points)
    left_k = jnp.where(valid & (index >= 1), kappa_ext[:-1], 0.0)
    right_k = jnp.where(valid & (index < total_points - 1), kappa_ext[1:], 0.0)
    react_v = jnp.where(valid, react_ext, 1.0)
    diag = left_k + right_k + react_v
    return left_k[:, None, None], right_k[:, None, None], diag[:, None, None]


def smooth(source, left_k, right_k, diag, halo):
    weights = omega_table(SWEEPS)
    state = weights[0] * source / diag
    for k in range(1, SWEEPS):
        padded = jnp.pad(state, ((1, 1), (0, 0), (0, 0)))
        applied = diag * state - left_k * padded[:-2] - right_k * padded[2:]
        state = state + weights[k] * (source - applied) / diag
    return state[halo : state.shape[0] - halo]


def local_coefficients(kappa, react):
    points = kappa.shape[0]
    total_points = points * lax.axis_size("sea")
    index = lax.axis_index("sea") * points + jnp.arange(points, dtype=jnp.int32)
    left_k = jnp.concatenate([jnp.zeros((1,), kappa.dtype), kappa[:-1]])
    right_k = jnp.where(index == total_points - 1, 0.0, kappa)
    diag = left_k + right_k + react
    return left_k[:, None, None], right_k[:, None, None], diag[:, None, None]


def banded_smooth(motion, coefficients, halo):
    points = motion.shape[0]
    width = 2 * halo + 1
    rows = jnp.arange(points, dtype=jnp.int32)
    lanes = jnp.arange(width, dtype=jnp.int32)
    probe = (rows[:, None] % width == lanes[None, :]).astype(jnp.float32)[:, None, :]
    response = smooth(probe, *coefficients, 0)[:, 0, :]
    picks = (rows[None, :, None] + lanes[:, None, None] - halo) % width == lanes[None, None, :]
    bands = lax.optimization_barrier(jnp.sum(jnp.where(picks, response[None], 0.0), axis=2))
    inner = points - 2 * halo
    total = None
    for offset in range(-halo, halo + 1):
        band = bands[offset + halo, halo : halo + inner][:, None, None]
        term = band * motion[halo + offset : halo + offset + inner].astype(jnp.float32)
        total = term if total is None else total + term
    return jnp.pad(total, ((halo, halo), (0, 0), (0, 0)))


def edge_rows(motion, halo_rows, coefficients, halo):
    points = motion.shape[0]
    span = 3 * halo + 1
    before, after = halo_rows
    left_src = jnp.concatenate([before, motion[: span - halo]]).astype(jnp.float32)
    right_src = jnp.concatenate([motion[points - span + halo :], after]).astype(jnp.float32)
    extent = coefficients[0].shape[0]
    steps = motion.shape[1]
    paired = [
        jnp.concatenate(
            [
                jnp.broadcast_to(vector[:span], (span, steps, 1)),
                jnp.broadcast_to(vector[extent - span :], (span, steps, 1)),
            ],
            axis=1,
        )
        for vector in coefficients
    ]
    both = smooth(jnp.concatenate([left_src, right_src], axis=1), *paired, halo)
    both = both.astype(jnp.bfloat16)
    return both[:, :steps], both[:, steps:]


def smooth_with_edges(motion, edges, local_coefficients_, halo, banded=False):
    points = motion.shape[0]
    keep = halo + 1
    if banded:
        interior = banded_smooth(motion, local_coefficients_, halo).astype(jnp.bfloat16)
    else:
        interior = smooth(motion.astype(jnp.float32), *local_coefficients_, 0).astype(jnp.bfloat16)
    left, right = edges
    interior = lax.dynamic_update_slice_in_dim(interior, left, 0, 0)
    return lax.dynamic_update_slice_in_dim(interior, right, points - keep, 0)


def dft_tables(steps_all):
    freq_ids = jnp.arange(steps_all, dtype=jnp.int32)
    phase_ids = freq_ids[:, None] * freq_ids[None, :] % steps_all
    angles = phase_ids.astype(jnp.float32) * (2.0 * math.pi / steps_all)
    scale = 1.0 / math.sqrt(steps_all)
    table = jnp.stack([jnp.cos(angles) * scale, -jnp.sin(angles) * scale], axis=1)
    table_high = lax.optimization_barrier(table.astype(jnp.bfloat16))
    table_low = (table - table_high.astype(jnp.float32)).astype(jnp.bfloat16)
    return table_high, table_low


def forward_chunk(prior_part, green, table_high, table_low):
    ways = lax.axis_size("tm")
    piece = lax.all_to_all(prior_part, "tm", split_axis=0, concat_axis=1, tiled=True)
    steps_all = piece.shape[1]
    high = table_high.reshape(ways, steps_all // ways, 2, steps_all)
    low = table_low.reshape(ways, steps_all // ways, 2, steps_all)
    spectrum = jnp.einsum("jfkt,qtc->jfkqc", high, piece, preferred_element_type=jnp.float32)
    spectrum = spectrum + jnp.einsum(
        "jfkt,qtc->jfkqc", low, piece, preferred_element_type=jnp.float32
    )
    spectrum = spectrum.astype(jnp.bfloat16)
    spectra = lax.all_to_all(spectrum, "tm", split_axis=0, concat_axis=0)
    real_s = spectra[:, :, 0]
    imag_s = spectra[:, :, 1]
    mixed = jnp.stack(
        [jnp.stack([real_s, imag_s], axis=2), jnp.stack([-imag_s, real_s], axis=2)], axis=0
    )
    blocks = green.reshape(green.shape[:3] + (ways, green.shape[3] // ways))
    partial = jnp.einsum("fksjq,kjfrqc->fsrc", blocks, mixed, preferred_element_type=jnp.float32)
    summed = lax.psum_scatter(partial.astype(jnp.bfloat16), "sea", scatter_dimension=1, tiled=True)
    return jnp.transpose(summed, (1, 0, 2, 3)).astype(jnp.float32)


def gathered_tables(blocks, steps_all):
    ways = lax.axis_size("tm")
    where_tm = lax.axis_index("tm").astype(jnp.int32)
    local = steps_all // ways
    freq_ids = where_tm * local + jnp.arange(local, dtype=jnp.int32)
    step_ids = (jnp.stack(blocks)[:, None] * local + jnp.arange(local, dtype=jnp.int32)).reshape(-1)
    phase_ids = freq_ids[:, None] * step_ids[None, :] % steps_all
    angles = phase_ids.astype(jnp.float32) * (2.0 * math.pi / steps_all)
    scale = 1.0 / math.sqrt(steps_all)
    real_w = jnp.cos(angles) * scale
    imag_w = -jnp.sin(angles) * scale
    table = jnp.stack(
        [jnp.stack([real_w, imag_w], axis=1), jnp.stack([-imag_w, real_w], axis=1)], axis=1
    )
    table_high = lax.optimization_barrier(table.astype(jnp.bfloat16))
    table_low = (table - table_high.astype(jnp.float32)).astype(jnp.bfloat16)
    return table_high, table_low


def gathered_spectrum(prior_part, after=None):
    where_tm = lax.axis_index("tm").astype(jnp.int32)
    chip_pairs = [(0, 1), (1, 0), (2, 3), (3, 2)]
    across = lax.ppermute(prior_part, "tm", [(0, 2), (2, 0), (1, 3), (3, 1)])
    partner = lax.ppermute(prior_part, "tm", chip_pairs)
    if after is not None:
        across, _ = lax.optimization_barrier((across, after))
    partner_across = lax.ppermute(across, "tm", chip_pairs)
    stacked = jnp.concatenate([prior_part, across, partner, partner_across], axis=1)
    blocks = [where_tm, where_tm ^ 2, where_tm ^ 1, where_tm ^ 3]
    steps_all = prior_part.shape[1] * len(blocks)
    table_high, _ = gathered_tables(blocks, steps_all)
    mixed = jnp.einsum("fkrt,ptc->fkrpc", table_high, stacked, preferred_element_type=jnp.float32)
    return mixed.astype(jnp.bfloat16)


def green_product(mixed, green):
    partial = jnp.einsum("fksp,fkrpc->fsrc", green, mixed, preferred_element_type=jnp.float32)
    summed = lax.psum_scatter(partial.astype(jnp.bfloat16), "sea", scatter_dimension=1, tiled=True)
    return jnp.transpose(summed, (1, 0, 2, 3)).astype(jnp.float32)


def on_device(motion, kappa, react, green):
    halo = SWEEPS - 1
    cols = motion.shape[2]
    width = cols // CHUNKS
    halo_rows, kappa_ext, react_ext = exchange_halo(motion, kappa, react, halo)
    coefficients = extended_coefficients(kappa_ext, react_ext, motion.shape[0], halo)
    inner = local_coefficients(kappa, react)
    left_all, right_all = edge_rows(motion, halo_rows, coefficients, halo)
    priors = []
    for c in range(CHUNKS):
        part = slice(c * width, (c + 1) * width)
        source = motion[:, :, part]
        if priors:
            source, _ = lax.optimization_barrier((source, priors[-1]))
        edges = (left_all[:, :, part], right_all[:, :, part])
        priors.append(smooth_with_edges(source, edges, inner, halo, c == 0))
    sensors = []
    if lax.axis_size("tm") == 4:
        spectra = []
        for c in range(CHUNKS):
            if c + 1 < CHUNKS:
                hold = (priors[c + 1],) + tuple(spectra[-1:])
            else:
                hold = tuple(spectra[-1:])
            mixed = gathered_spectrum(priors[c], hold if hold else None)
            spectra.append(mixed)
            sensors.append(green_product(mixed, green))
    else:
        table_high, table_low = dft_tables(motion.shape[1] * lax.axis_size("tm"))
        for prior_part in priors:
            sensors.append(forward_chunk(prior_part, green, table_high, table_low))
    return (jnp.concatenate(priors, axis=2), jnp.concatenate(sensors, axis=3))


def solution(mesh):
    in_specs = (P("sea", "tm", None), P("sea"), P("sea"), P("tm", None, None, "sea"))
    out_specs = (P("sea", "tm", None), P("sea", "tm", None, None))
    return jax.shard_map(
        on_device, mesh=mesh, in_specs=in_specs, out_specs=out_specs, check_vma=False
    )
```
